512 devices in a mesh: ctx: 64 (over z_lo, y, core), wa: 8 (over z_hi, x).
Axes of the slice: x: 4, y: 4, z: 16 (z_hi: 2, z_lo: 8; z = z_hi * 8 + z_lo), core: 2. Of those that a mesh axis runs over, the one named last changes fastest.
Arguments:
- q_nope: bfloat16 [512, 8192], P('ctx', 'wa'), may hold values from -6 to 6
- q_rope: bfloat16 [512, 4096], P('ctx', 'wa'), may hold values from -100 to 100
- w_uk: bfloat16 [64, 128, 512], P('wa'), may hold values from -0.25 to 0.25
- w_uv: bfloat16 [64, 512, 128], P('wa'), may hold values from -0.25 to 0.25
- cache: bfloat16 [32768, 576], P('ctx'), may hold values from -16 to 16
- cache_scale: float32 [32768], P('ctx'), may hold values from 0.5 to 2, as said below
- new_latent: bfloat16 [512, 576], P('ctx'), may hold values from -16 to 16
- cache_doc: int32 [512], P('ctx'), may hold values from 0 to 15
- new_lengths: int32 [16], replicated, may hold values from 1 to 128, 512 in all
Outputs:
- attn_out: bfloat16 [512, 8192], P('ctx', 'wa')
The draws below stay inside these ranges and needn't reach their ends.
Inputs may be any that keep to these rules, and one draw needn't show every extreme that they name: `cache_scale`: each scale is 0.5, 1 or 2.
All inputs are finite; a program needn't handle non-finite values.
Results may differ from the reference program's by a relative error of at most 0.0064.
Values may be sent and summed in bfloat16 or wider, within the bound.
No kernel may reach another device: no remote copies, remote signals or barrier semaphores. Data moves between devices by JAX's collectives and lax.ppermute only.
A program may use at most 64 MiB of HBM per device.

```python
import math
import jax
import jax.numpy as jnp
import numpy as np
from jax import lax

LATENT = 512
ROPE = 64
NOPE = 128
VDIM = 128
HEADS = 64
BLK = 64
DOCS = 16
TOK_DEV = 8
CACHE_DEV = 512
NEW = 512
CACHE = 32768
CBLOCKS = 512
N_CTX = 64


def drawn_rows(key, rows):
    drawn = jnp.clip(jax.random.normal(jax.random.fold_in(key, 11), (rows, LATENT + ROPE), jnp.float32), -6.0, 6.0)
    return drawn.astype(jnp.bfloat16)


def draw_cache(key, part):
    return drawn_rows(jax.random.fold_in(key, 101), CACHE)


def draw_new_latent(key, part):
    return drawn_rows(jax.random.fold_in(key, 202), NEW)


def draw_cache_scale(key, part):
    level = jax.random.randint(jax.random.fold_in(key, 303), (CACHE,), 0, 3)
    return jnp.where(level == 0, 0.5, jnp.where(level == 1, 1.0, 2.0)).astype(jnp.float32)


def draw_q_rope(key, part):
    drawn = jnp.clip(jax.random.normal(jax.random.fold_in(key, 23), (NEW, HEADS * ROPE), jnp.float32), -6.0, 6.0)
    return drawn.astype(jnp.bfloat16)


def set_ends(result, rng, smallest, largest):
    spot = [jax.random.randint(jax.random.fold_in(rng, axis), (), 0, length) for axis, length in enumerate(result.shape)]
    main_axis = result.shape.index(max(result.shape))
    next_to = spot[:main_axis] + [(spot[main_axis] + 1) % result.shape[main_axis]] + spot[main_axis + 1:]
    return result.at[tuple(spot)].set(smallest).at[tuple(next_to)].set(largest)


def shard_levels(rng, dims, split, least, top_value):
    level = 1.0
    for dim, parts in split:
        draws = jax.random.uniform(jax.random.fold_in(jax.random.fold_in(rng, 6), dim), (parts,), jnp.float32, least / len(split), top_value / len(split))
        level = level * jnp.repeat(jnp.exp(draws), dims[dim] // parts).reshape((-1,) + (1,) * (len(dims) - 1 - dim))
    return level


def rank_bounds(number_of, lean):
    portions = [(1 << 20) // math.isqrt(grade ** lean) + 1 for grade in range(1, number_of + 1)]
    scale = 1 + sum(portions) // (1 << 30)
    return np.cumsum(np.array([max(1, weight // scale) for weight in portions]))


def ranked(own_key, dims, count, skew):
    listing = rank_bounds(count, skew)
    ticket = jax.random.randint(jax.random.fold_in(own_key, 1), dims, 0, int(listing[count - 1]))
    rank = jnp.searchsorted(jnp.asarray(listing, jnp.int32), ticket, side="right")
    return jax.random.permutation(jax.random.fold_in(own_key, 2), count)[rank].astype(jnp.int32)


def split_up(count, total, reach, skew):
    weights = [(1 << 20) // math.isqrt(standing ** skew) + 1 for standing in range(2, count + 1)]
    rest, given = total - reach - (count - 1), [1] * (count - 1)
    while rest > 0:
        free = [i for i in range(count - 1) if given[i] < reach]
        whole, remaining = sum([weights[i] for i in free]), rest
        for i in free:
            more = min(reach - given[i], max(1, remaining * weights[i] // whole), rest)
            given[i] = given[i] + more
            rest = rest - more
    return np.array([reach] + given)


def ragged_sizes(stream_key, number_of, total, reach, skew):
    if number_of == 2:
        one = jax.random.randint(stream_key, (), max(1, total - reach), min(reach, total - 1) + 1)
        return jnp.stack([one, total - one])
    lengths = jnp.asarray(split_up(number_of, total, reach, skew), jnp.int32)
    couples = (number_of - 1) // 2
    giver, taker = lengths[1:1 + 2 * couples:2], lengths[2:2 + 2 * couples:2]
    room = jnp.minimum(giver - 1, reach - taker)
    shifted = jax.random.randint(jax.random.fold_in(stream_key, 1), (couples,), 0, 1 << 20) % (room + 1)
    lengths = lengths.at[1:1 + 2 * couples:2].set(giver - shifted).at[2:2 + 2 * couples:2].set(taker + shifted)
    return lengths[jax.random.permutation(jax.random.fold_in(stream_key, 2), number_of)]


def normal_values(stream_key, extent, scale, reach, shards=(), kind=jnp.bfloat16):
    gain = shard_levels(stream_key, extent, shards, -0.22, 0.18) if shards else 1.0
    entries = jax.random.normal(stream_key, extent, jnp.float32) * scale * gain
    return jnp.minimum(jnp.maximum(entries, -reach), reach).astype(kind)


def setup_inputs(seed: int = 0) -> dict:
    seeds = jax.random.split(jax.random.key(seed), 10)
    q_nope = normal_values(seeds[0], (NEW, HEADS * NOPE), 1.0, 6.0, ((0, 64), (1, 8)))
    q_rope = draw_q_rope(jax.random.fold_in(seeds[9], 71), 0)
    w_uk = normal_values(seeds[2], (HEADS, NOPE, LATENT), LATENT ** -0.5, 0.25, ((0, 8),))
    w_uv = normal_values(seeds[3], (HEADS, LATENT, VDIM), LATENT ** -0.5, 0.25, ((0, 8),))
    cache = draw_cache(jax.random.fold_in(seeds[9], 71), 0)
    cache_scale = draw_cache_scale(jax.random.fold_in(seeds[9], 71), 0)
    new_latent = draw_new_latent(jax.random.fold_in(seeds[9], 71), 0)
    cache_doc = set_ends(ranked(seeds[7], (CBLOCKS,), DOCS, 2), jax.random.fold_in(seeds[7], 3), 0, DOCS - 1).astype(jnp.int32)
    new_lengths = ragged_sizes(seeds[8], DOCS, NEW, NEW // 4, 2).astype(jnp.int32)
    return {"q_nope": q_nope, "q_rope": q_rope, "w_uk": w_uk, "w_uv": w_uv, "cache": cache, "cache_scale": cache_scale, "new_latent": new_latent, "cache_doc": cache_doc, "new_lengths": new_lengths}


def doc_index(position, new_lengths):
    ends = jnp.cumsum(new_lengths).astype(jnp.int32)
    return jnp.sum((ends[None, :] <= position[:, None]).astype(jnp.int32), axis=1).astype(jnp.int32)


def reference(q_nope, q_rope, w_uk, w_uv, cache, cache_scale, new_latent, cache_doc, new_lengths):
    score_scale = (NOPE + ROPE) ** -0.5
    nope_rows = q_nope.astype(jnp.float32).reshape(NEW, HEADS, NOPE)
    q_lat = jnp.einsum("thn,hnl->thl", nope_rows, w_uk.astype(jnp.float32)).astype(jnp.bfloat16)
    q_lat = lax.optimization_barrier(q_lat)
    query = jnp.concatenate([q_lat, q_rope.reshape(NEW, HEADS, ROPE)], axis=2).astype(jnp.float32)
    dequant = (cache.astype(jnp.float32) * cache_scale[:, None]).astype(jnp.bfloat16)
    dequant = lax.optimization_barrier(dequant)
    query_pos = jnp.arange(NEW, dtype=jnp.int32)
    query_doc = doc_index(query_pos, new_lengths)
    cached_doc = jnp.repeat(cache_doc, BLK).astype(jnp.int32)
    width = LATENT + ROPE
    shard_keys = jnp.concatenate([dequant.reshape(N_CTX, CACHE_DEV, width), new_latent.reshape(N_CTX, TOK_DEV, width)], axis=1)
    shard_docs = jnp.concatenate([cached_doc.reshape(N_CTX, CACHE_DEV), query_doc.reshape(N_CTX, TOK_DEV)], axis=1)
    cached_pos = jnp.full((N_CTX, CACHE_DEV), -1, dtype=jnp.int32)
    shard_pos = jnp.concatenate([cached_pos, query_pos.reshape(N_CTX, TOK_DEV)], axis=1)
    w_value = w_uv.astype(jnp.float32)

    def masked_scores(key_rows, key_doc, key_pos):
        score = jnp.einsum("qhl,kl->qhk", query, key_rows.astype(jnp.float32)) * score_scale
        allowed = (query_doc[:, None] == key_doc[None, :]) & (key_pos[None, :] <= query_pos[:, None])
        return jnp.where(allowed[:, None, :], score, -jnp.inf)

    def shard_max(packed):
        return jnp.max(masked_scores(packed[0], packed[1], packed[2]), axis=2)

    maxima = lax.map(shard_max, (shard_keys, shard_docs, shard_pos))
    row_max = jnp.max(maxima, axis=0)

    def accumulate(carry, packed):
        numer, total = carry
        score = masked_scores(packed[0], packed[1], packed[2])
        local = packed[3]
        shift = jnp.where(jnp.isfinite(local), local, jnp.zeros_like(local))
        factor = jnp.exp(local - row_max)
        weight = jnp.exp(score - shift[:, :, None])
        total = total + factor * jnp.sum(weight, axis=2)
        weight_low = lax.optimization_barrier(weight.astype(jnp.bfloat16)).astype(jnp.float32)
        latent_keys = packed[0][:, :LATENT].astype(jnp.float32)
        part_lat = jnp.einsum("qhk,kl->qhl", weight_low, latent_keys).astype(jnp.bfloat16)
        part_lat = lax.optimization_barrier(part_lat).astype(jnp.float32)
        numer = numer + factor[:, :, None] * jnp.einsum("qhl,hlv->qhv", part_lat, w_value)
        return (numer, total), None

    start = (jnp.zeros((NEW, HEADS, VDIM), jnp.float32), jnp.zeros((NEW, HEADS), jnp.float32))
    (numer, total), unused = lax.scan(accumulate, start, (shard_keys, shard_docs, shard_pos, maxima))
    return (numer / total[:, :, None]).astype(jnp.bfloat16).reshape(NEW, HEADS * VDIM)
```

```python
import jax
import jax.numpy as jnp
from jax import lax
from jax.sharding import PartitionSpec as P


def doc_index(position, new_lengths):
    ends = jnp.cumsum(new_lengths)
    return jnp.sum((ends[None, :] <= position[:, None]).astype(jnp.int32), axis=1)


def absorb_rows(nope_rows, w_uk):
    row_count = nope_rows.shape[0]
    heads_dev, nope_dim, latent_dim = w_uk.shape
    shaped = nope_rows.reshape(row_count, heads_dev, nope_dim)
    absorbed = jnp.einsum("thn,hnl->thl", shaped, w_uk, preferred_element_type=jnp.float32)
    return absorbed.astype(jnp.bfloat16)


def body(q_nope, q_rope, w_uk, w_uv, cache, cache_scale, new_latent, cache_doc, new_lengths):
    tok_rows = q_nope.shape[0]
    heads_dev, nope_dim, latent_dim = w_uk.shape
    value_dim = w_uv.shape[2]
    rope_dim = q_rope.shape[1] // heads_dev
    shards = lax.axis_size("ctx")
    all_rows = tok_rows * shards
    my_index = lax.axis_index("ctx")
    score_scale = (nope_dim + rope_dim) ** (-0.5)
    own_q = jnp.concatenate([q_nope, q_rope], axis=1)
    all_q = lax.all_gather(own_q, "ctx", axis=0, tiled=True)
    nope_width = heads_dev * nope_dim
    all_lat = absorb_rows(all_q[:, :nope_width], w_uk)
    all_rope = all_q[:, nope_width:]
    query = jnp.concatenate(
        [all_lat, all_rope.reshape(all_rows, heads_dev, rope_dim)],
        axis=2,
    )
    dequant = (cache.astype(jnp.float32) * cache_scale[:, None]).astype(jnp.bfloat16)
    key_rows = jnp.concatenate([dequant, new_latent], axis=0)
    cache_len = cache.shape[0]
    block_len = cache_len // cache_doc.shape[0]
    query_pos = jnp.arange(all_rows, dtype=jnp.int32)
    query_doc = doc_index(query_pos, new_lengths)
    new_pos = my_index * tok_rows + jnp.arange(tok_rows, dtype=jnp.int32)
    key_doc = jnp.concatenate([jnp.repeat(cache_doc, block_len), doc_index(new_pos, new_lengths)])
    key_pos = jnp.concatenate([jnp.full((cache_len,), -1, dtype=jnp.int32), new_pos])
    allowed = (query_doc[:, None] == key_doc[None, :]) & (key_pos[None, :] <= query_pos[:, None])
    score = (
        jnp.einsum("qhl,kl->qhk", query, key_rows, preferred_element_type=jnp.float32) * score_scale
    )
    masked = jnp.where(allowed[:, None, :], score, -jnp.inf)
    local_max = jnp.max(masked, axis=2)
    shift = jnp.where(jnp.isfinite(local_max), local_max, jnp.zeros_like(local_max))
    weight = jnp.exp(masked - shift[:, :, None])
    totals = jnp.sum(weight, axis=2)
    weight_low = weight.astype(jnp.bfloat16)
    part_lat = jnp.einsum(
        "qhk,kl->qhl", weight_low, key_rows[:, :latent_dim], preferred_element_type=jnp.float32
    ).astype(jnp.bfloat16)
    numerator = jnp.einsum("qhl,hlv->qhv", part_lat, w_uv, preferred_element_type=jnp.float32)
    stats = lax.all_gather(jnp.concatenate([local_max, totals], axis=1), "ctx", axis=0, tiled=False)
    row_max = jnp.max(stats[:, :, :heads_dev], axis=0)
    factor = jnp.exp(local_max - row_max)
    scaled = (numerator * factor[:, :, None]).reshape(all_rows, heads_dev * value_dim)
    own_numer = lax.psum_scatter(scaled, "ctx", scatter_dimension=0, tiled=True)
    own_numer = own_numer.reshape(tok_rows, heads_dev, value_dim)
    own_stats = lax.dynamic_slice_in_dim(stats, my_index * tok_rows, tok_rows, axis=1)
    own_max = lax.dynamic_slice_in_dim(row_max, my_index * tok_rows, tok_rows, axis=0)
    own_factor = jnp.exp(own_stats[:, :, :heads_dev] - own_max[None])
    own_total = jnp.sum(own_factor * own_stats[:, :, heads_dev:], axis=0)
    result = own_numer / own_total[:, :, None]
    return result.astype(jnp.bfloat16).reshape(tok_rows, heads_dev * value_dim)


def solution(mesh):
    placed = (
        P("ctx", "wa"),
        P("ctx", "wa"),
        P("wa", None, None),
        P("wa", None, None),
        P("ctx", None),
        P("ctx"),
        P("ctx", None),
        P("ctx"),
        P(),
    )
    return jax.shard_map(
        body, mesh=mesh, in_specs=placed, out_specs=P("ctx", "wa"), check_vma=False
    )
```

```python
import jax
import jax.numpy as jnp
import numpy as np
from jax import lax
from jax.sharding import Mesh, PartitionSpec as P

CTX_PARTS = ("cz", "cy", "cc")


def doc_index(position, new_lengths):
    ends = jnp.cumsum(new_lengths)
    return jnp.sum((ends[None, :] <= position[:, None]).astype(jnp.int32), axis=1)


def absorb_rows(nope_rows, w_uk):
    row_count = nope_rows.shape[0]
    heads_dev, nope_dim, latent_dim = w_uk.shape
    shaped = nope_rows.reshape(row_count, heads_dev, nope_dim)
    absorbed = jnp.einsum("thn,hnl->thl", shaped, w_uk, preferred_element_type=jnp.float32)
    return absorbed.astype(jnp.bfloat16)


def ctx_index():
    index = lax.axis_index(CTX_PARTS[0])
    for name in CTX_PARTS[1:]:
        index = index * lax.axis_size(name) + lax.axis_index(name)
    return index


def gather_rows(x):
    for name in reversed(CTX_PARTS):
        x = lax.all_gather(x, name, axis=0, tiled=True)
    return x


def scatter_rows(x):
    for name in CTX_PARTS:
        x = lax.psum_scatter(x, name, scatter_dimension=0, tiled=True)
    return x


def merge_stats(stats, heads_dev):
    for name in reversed(CTX_PARTS):
        group = lax.all_gather(stats, name, axis=0, tiled=False)
        peak = jnp.max(group[:, :, :heads_dev], axis=0)
        shifted = jnp.where(jnp.isfinite(peak), peak, jnp.zeros_like(peak))
        scale = jnp.exp(group[:, :, :heads_dev] - shifted[None])
        total = jnp.sum(scale * group[:, :, heads_dev:], axis=0)
        stats = jnp.concatenate([peak, total], axis=1)
    return stats[:, :heads_dev], stats[:, heads_dev:]


def body(q_nope, q_rope, w_uk, w_uv, cache, cache_scale, new_latent, cache_doc, new_lengths):
    tok_rows = q_nope.shape[0]
    heads_dev, nope_dim, latent_dim = w_uk.shape
    value_dim = w_uv.shape[2]
    rope_dim = q_rope.shape[1] // heads_dev
    shards = 1
    for name in CTX_PARTS:
        shards = shards * lax.axis_size(name)
    all_rows = tok_rows * shards
    my_index = ctx_index()
    score_scale = (nope_dim + rope_dim) ** (-0.5)
    own_q = jnp.concatenate([q_nope, q_rope], axis=1)
    all_q = gather_rows(own_q)
    nope_width = heads_dev * nope_dim
    all_lat = absorb_rows(all_q[:, :nope_width], w_uk)
    all_rope = all_q[:, nope_width:]
    query = jnp.concatenate(
        [all_lat, all_rope.reshape(all_rows, heads_dev, rope_dim)],
        axis=2,
    )
    dequant = (cache.astype(jnp.float32) * cache_scale[:, None]).astype(jnp.bfloat16)
    key_rows = jnp.concatenate([dequant, new_latent], axis=0)
    cache_len = cache.shape[0]
    block_len = cache_len // cache_doc.shape[0]
    query_pos = jnp.arange(all_rows, dtype=jnp.int32)
    query_doc = doc_index(query_pos, new_lengths)
    new_pos = my_index * tok_rows + jnp.arange(tok_rows, dtype=jnp.int32)
    key_doc = jnp.concatenate([jnp.repeat(cache_doc, block_len), doc_index(new_pos, new_lengths)])
    key_pos = jnp.concatenate([jnp.full((cache_len,), -1, dtype=jnp.int32), new_pos])
    allowed = (query_doc[:, None] == key_doc[None, :]) & (key_pos[None, :] <= query_pos[:, None])
    score = (
        jnp.einsum("qhl,kl->qhk", query, key_rows, preferred_element_type=jnp.float32) * score_scale
    )
    masked = jnp.where(allowed[:, None, :], score, -jnp.inf)
    local_max = jnp.max(masked, axis=2)
    shift = jnp.where(jnp.isfinite(local_max), local_max, jnp.zeros_like(local_max))
    weight = jnp.exp(masked - shift[:, :, None])
    totals = jnp.sum(weight, axis=2)
    weight_low = weight.astype(jnp.bfloat16)
    part_lat = jnp.einsum(
        "qhk,kl->qhl", weight_low, key_rows[:, :latent_dim], preferred_element_type=jnp.float32
    ).astype(jnp.bfloat16)
    numerator = jnp.einsum("qhl,hlv->qhv", part_lat, w_uv, preferred_element_type=jnp.float32)
    row_max, row_total = merge_stats(jnp.concatenate([local_max, totals], axis=1), heads_dev)
    factor = jnp.exp(local_max - row_max)
    scaled = (numerator * factor[:, :, None]).reshape(all_rows, heads_dev * value_dim)
    own_numer = scatter_rows(scaled).reshape(tok_rows, heads_dev, value_dim)
    own_total = lax.dynamic_slice_in_dim(row_total, my_index * tok_rows, tok_rows, axis=0)
    result = own_numer / own_total[:, :, None]
    return result.astype(jnp.bfloat16).reshape(tok_rows, heads_dev * value_dim)


def solution(mesh):
    ctx_shape = (8, 4, 2)
    grid = np.asarray(mesh.devices).reshape(ctx_shape + (mesh.shape["wa"],))
    fine = Mesh(grid, CTX_PARTS + ("wa",))
    rows = CTX_PARTS
    placed = (
        P(rows, "wa"),
        P(rows, "wa"),
        P("wa", None, None),
        P("wa", None, None),
        P(rows, None),
        P(rows),
        P(rows, None),
        P(rows),
        P(),
    )
    return jax.shard_map(
        body, mesh=fine, in_specs=placed, out_specs=P(rows, "wa"), check_vma=False
    )
```

```python
import jax
import jax.numpy as jnp
import numpy as np
from jax import lax
from jax.sharding import Mesh, PartitionSpec as P

CHIP_PARTS = ("cz", "cy")
CORE = "cc"


def doc_index(position, new_lengths):
    ends = jnp.cumsum(new_lengths)
    return jnp.sum((ends[None, :] <= position[:, None]).astype(jnp.int32), axis=1)


def absorb_rows(nope_rows, w_uk):
    row_count = nope_rows.shape[0]
    heads_dev, nope_dim, latent_dim = w_uk.shape
    shaped = nope_rows.reshape(row_count, heads_dev, nope_dim)
    absorbed = jnp.einsum("thn,hnl->thl", shaped, w_uk, preferred_element_type=jnp.float32)
    return absorbed.astype(jnp.bfloat16)


def chip_index():
    index = lax.axis_index(CHIP_PARTS[0])
    for name in CHIP_PARTS[1:]:
        index = index * lax.axis_size(name) + lax.axis_index(name)
    return index


def gather_rows(x):
    for name in reversed(CHIP_PARTS):
        x = lax.all_gather(x, name, axis=0, tiled=True)
    return x


def scatter_rows(x):
    for name in CHIP_PARTS:
        x = lax.psum_scatter(x, name, scatter_dimension=0, tiled=True)
    return x


def merge_stats(stats, heads_dev):
    for name in reversed(CHIP_PARTS):
        group = lax.all_gather(stats, name, axis=0, tiled=False)
        peak = jnp.max(group[:, :, :heads_dev], axis=0)
        shifted = jnp.where(jnp.isfinite(peak), peak, jnp.zeros_like(peak))
        scale = jnp.exp(group[:, :, :heads_dev] - shifted[None])
        total = jnp.sum(scale * group[:, :, heads_dev:], axis=0)
        stats = jnp.concatenate([peak, total], axis=1)
    return stats[:, :heads_dev], stats[:, heads_dev:]


def swap_cores(x):
    return lax.ppermute(x, CORE, [(0, 1), (1, 0)])


def body(q_nope, q_rope, w_uk, w_uv, cache, cache_scale, new_latent, cache_doc, new_lengths):
    tok_rows = q_nope.shape[0]
    heads_dev, nope_dim, latent_dim = w_uk.shape
    value_dim = w_uv.shape[2]
    rope_dim = q_rope.shape[1] // heads_dev
    cores = lax.axis_size(CORE)
    chips = 1
    for name in CHIP_PARTS:
        chips = chips * lax.axis_size(name)
    q_rows = tok_rows * chips
    my_chip = chip_index()
    my_core = lax.axis_index(CORE)
    other_core = 1 - my_core
    score_scale = (nope_dim + rope_dim) ** (-0.5)

    dequant = (cache.astype(jnp.float32) * cache_scale[:, None]).astype(jnp.bfloat16)
    own_keys = jnp.concatenate([dequant, new_latent], axis=0)
    other_keys = swap_cores(own_keys)
    other_doc = swap_cores(cache_doc)

    own_q = jnp.concatenate([q_nope, q_rope], axis=1)
    all_q = gather_rows(own_q)
    nope_width = heads_dev * nope_dim
    all_lat = absorb_rows(all_q[:, :nope_width], w_uk)
    all_rope = all_q[:, nope_width:]
    query = jnp.concatenate(
        [all_lat, all_rope.reshape(q_rows, heads_dev, rope_dim)],
        axis=2,
    )
    cache_len = cache.shape[0]
    block_len = cache_len // cache_doc.shape[0]
    row = jnp.arange(q_rows, dtype=jnp.int32)
    query_pos = ((row // tok_rows) * cores + my_core) * tok_rows + row % tok_rows
    query_doc = doc_index(query_pos, new_lengths)

    def key_meta(core, docs):
        new_pos = (my_chip * cores + core) * tok_rows + jnp.arange(tok_rows, dtype=jnp.int32)
        key_doc = jnp.concatenate([jnp.repeat(docs, block_len), doc_index(new_pos, new_lengths)])
        key_pos = jnp.concatenate([jnp.full((cache_len,), -1, dtype=jnp.int32), new_pos])
        return key_doc, key_pos

    own_doc, own_pos = key_meta(my_core, cache_doc)
    far_doc, far_pos = key_meta(other_core, other_doc)
    key_rows = jnp.concatenate([own_keys, other_keys], axis=0)
    key_doc = jnp.concatenate([own_doc, far_doc])
    key_pos = jnp.concatenate([own_pos, far_pos])
    allowed = (query_doc[:, None] == key_doc[None, :]) & (key_pos[None, :] <= query_pos[:, None])
    score = (
        jnp.einsum("qhl,kl->qhk", query, key_rows, preferred_element_type=jnp.float32) * score_scale
    )
    masked = jnp.where(allowed[:, None, :], score, -jnp.inf)
    local_max = jnp.max(masked, axis=2)
    shift = jnp.where(jnp.isfinite(local_max), local_max, jnp.zeros_like(local_max))
    weight = jnp.exp(masked - shift[:, :, None])
    totals = jnp.sum(weight, axis=2)
    weight_low = weight.astype(jnp.bfloat16)
    part_lat = jnp.einsum(
        "qhk,kl->qhl", weight_low, key_rows[:, :latent_dim], preferred_element_type=jnp.float32
    ).astype(jnp.bfloat16)
    numerator = jnp.einsum("qhl,hlv->qhv", part_lat, w_uv, preferred_element_type=jnp.float32)
    row_max, row_total = merge_stats(jnp.concatenate([local_max, totals], axis=1), heads_dev)
    factor = jnp.exp(local_max - row_max)
    scaled = (numerator * factor[:, :, None]).reshape(q_rows, heads_dev * value_dim)
    own_numer = scatter_rows(scaled).reshape(tok_rows, heads_dev, value_dim)
    own_total = lax.dynamic_slice_in_dim(row_total, my_chip * tok_rows, tok_rows, axis=0)
    result = own_numer / own_total[:, :, None]
    return result.astype(jnp.bfloat16).reshape(tok_rows, heads_dev * value_dim)


def solution(mesh):
    ctx_shape = (8, 4, 2)
    grid = np.asarray(mesh.devices).reshape(ctx_shape + (mesh.shape["wa"],))
    fine = Mesh(grid, CHIP_PARTS + (CORE, "wa"))
    rows = CHIP_PARTS + (CORE,)
    placed = (
        P(rows, "wa"),
        P(rows, "wa"),
        P("wa", None, None),
        P("wa", None, None),
        P(rows, None),
        P(rows),
        P(rows, None),
        P(rows),
        P(),
    )
    return jax.shard_map(
        body, mesh=fine, in_specs=placed, out_specs=P(rows, "wa"), check_vma=False
    )
```

```python
import jax
import jax.numpy as jnp
import numpy as np
from jax import lax
from jax.sharding import Mesh, PartitionSpec as P

CHIP_PARTS = ("cz", "cy")
CORE = "cc"


def doc_index(position, new_lengths):
    ends = jnp.cumsum(new_lengths)
    return jnp.sum((ends[None, :] <= position[:, None]).astype(jnp.int32), axis=1)


def absorb_rows(nope_rows, w_uk):
    row_count = nope_rows.shape[0]
    heads_dev, nope_dim, latent_dim = w_uk.shape
    shaped = nope_rows.reshape(row_count, heads_dev, nope_dim)
    absorbed = jnp.einsum("thn,hnl->thl", shaped, w_uk, preferred_element_type=jnp.float32)
    return absorbed.astype(jnp.bfloat16)


def chip_index():
    return lax.axis_index("cz") * lax.axis_size("cy") + lax.axis_index("cy")


def shift_pairs(count, step):
    return [(i, (i - step) % count) for i in range(count)]


def gather_blocks(x, name):
    count = lax.axis_size(name)
    me = lax.axis_index(name)
    got = [x] + [lax.ppermute(x, name, shift_pairs(count, step)) for step in range(1, count)]
    return jnp.roll(jnp.stack(got), me, axis=0)


def spread_blocks(x, name):
    count = lax.axis_size(name)
    me = lax.axis_index(name)
    got = [x[me]]
    for step in range(1, count):
        got.append(lax.ppermute(x[(me - step) % count], name, shift_pairs(count, step)))
    return jnp.stack(got)


def merge_parts(parts, heads_dev, value_dim):
    width = heads_dev * value_dim
    numer = parts[:, :, :width]
    peaks = parts[:, :, width : width + heads_dev]
    sums = parts[:, :, width + heads_dev :]
    peak = jnp.max(peaks, axis=0)
    shifted = jnp.where(jnp.isfinite(peak), peak, jnp.zeros_like(peak))
    scale = jnp.exp(peaks - shifted[None])
    count, rows = parts.shape[0], parts.shape[1]
    numer = numer.reshape(count, rows, heads_dev, value_dim) * scale[:, :, :, None]
    numer = jnp.sum(numer, axis=0).reshape(rows, width)
    total = jnp.sum(scale * sums, axis=0)
    return jnp.concatenate([numer, peak, total], axis=1)


def reduce_rows(x, heads_dev, value_dim):
    for name in ("cy", "cz"):
        count = lax.axis_size(name)
        blocks = x.reshape((count, x.shape[0] // count) + x.shape[1:])
        x = merge_parts(spread_blocks(blocks, name), heads_dev, value_dim)
    return x


def swap_cores(x):
    return lax.ppermute(x, CORE, [(0, 1), (1, 0)])


def body(q_nope, q_rope, w_uk, w_uv, cache, cache_scale, new_latent, cache_doc, new_lengths):
    tok_rows = q_nope.shape[0]
    heads_dev, nope_dim, latent_dim = w_uk.shape
    value_dim = w_uv.shape[2]
    rope_dim = q_rope.shape[1] // heads_dev
    cores = lax.axis_size(CORE)
    chips = 1
    for name in CHIP_PARTS:
        chips = chips * lax.axis_size(name)
    q_rows = tok_rows * chips
    my_chip = chip_index()
    my_core = lax.axis_index(CORE)
    other_core = 1 - my_core
    score_scale = (nope_dim + rope_dim) ** (-0.5)

    dequant = (cache.astype(jnp.float32) * cache_scale[:, None]).astype(jnp.bfloat16)
    own_keys = jnp.concatenate([dequant, new_latent], axis=0)
    other_keys = swap_cores(own_keys)
    other_doc = swap_cores(cache_doc)

    own_q = jnp.concatenate([q_nope, q_rope], axis=1)
    all_q = gather_blocks(own_q, "cz").reshape(-1, own_q.shape[1])
    all_q = gather_blocks(all_q, "cy").reshape(-1, own_q.shape[1])
    nope_width = heads_dev * nope_dim
    all_lat = absorb_rows(all_q[:, :nope_width], w_uk)
    all_rope = all_q[:, nope_width:]
    query = jnp.concatenate(
        [all_lat, all_rope.reshape(q_rows, heads_dev, rope_dim)],
        axis=2,
    )
    cache_len = cache.shape[0]
    block_len = cache_len // cache_doc.shape[0]
    row = jnp.arange(q_rows, dtype=jnp.int32)
    z_count = lax.axis_size("cz")
    row_chip = (row // tok_rows) % z_count * lax.axis_size("cy") + row // (tok_rows * z_count)
    query_pos = (row_chip * cores + my_core) * tok_rows + row % tok_rows
    query_doc = doc_index(query_pos, new_lengths)

    def key_meta(core, docs):
        new_pos = (my_chip * cores + core) * tok_rows + jnp.arange(tok_rows, dtype=jnp.int32)
        key_doc = jnp.concatenate([jnp.repeat(docs, block_len), doc_index(new_pos, new_lengths)])
        key_pos = jnp.concatenate([jnp.full((cache_len,), -1, dtype=jnp.int32), new_pos])
        return key_doc, key_pos

    own_doc, own_pos = key_meta(my_core, cache_doc)
    far_doc, far_pos = key_meta(other_core, other_doc)
    key_rows = jnp.concatenate([own_keys, other_keys], axis=0)
    key_doc = jnp.concatenate([own_doc, far_doc])
    key_pos = jnp.concatenate([own_pos, far_pos])
    allowed = (query_doc[:, None] == key_doc[None, :]) & (key_pos[None, :] <= query_pos[:, None])
    score = (
        jnp.einsum("qhl,kl->qhk", query, key_rows, preferred_element_type=jnp.float32) * score_scale
    )
    masked = jnp.where(allowed[:, None, :], score, -jnp.inf)
    local_max = jnp.max(masked, axis=2)
    shift = jnp.where(jnp.isfinite(local_max), local_max, jnp.zeros_like(local_max))
    weight = jnp.exp(masked - shift[:, :, None])
    totals = jnp.sum(weight, axis=2)
    weight_low = weight.astype(jnp.bfloat16)
    part_lat = jnp.einsum(
        "qhk,kl->qhl", weight_low, key_rows[:, :latent_dim], preferred_element_type=jnp.float32
    ).astype(jnp.bfloat16)
    numerator = jnp.einsum("qhl,hlv->qhv", part_lat, w_uv, preferred_element_type=jnp.float32)
    width = heads_dev * value_dim
    parts = jnp.concatenate([numerator.reshape(q_rows, width), local_max, totals], axis=1)
    merged = reduce_rows(parts, heads_dev, value_dim)
    own_numer = merged[:, :width].reshape(tok_rows, heads_dev, value_dim)
    own_total = merged[:, width + heads_dev :]
    result = own_numer / own_total[:, :, None]
    return result.astype(jnp.bfloat16).reshape(tok_rows, heads_dev * value_dim)


def solution(mesh):
    ctx_shape = (8, 4, 2)
    grid = np.asarray(mesh.devices).reshape(ctx_shape + (mesh.shape["wa"],))
    fine = Mesh(grid, CHIP_PARTS + (CORE, "wa"))
    rows = CHIP_PARTS + (CORE,)
    placed = (
        P(rows, "wa"),
        P(rows, "wa"),
        P("wa", None, None),
        P("wa", None, None),
        P(rows, None),
        P(rows),
        P(rows, None),
        P(rows),
        P(),
    )
    return jax.shard_map(
        body, mesh=fine, in_specs=placed, out_specs=P(rows, "wa"), check_vma=False
    )
```

```python
import jax
import jax.numpy as jnp
import numpy as np
from jax import lax
from jax.sharding import Mesh, PartitionSpec as P

CHIP_PARTS = ("cz", "cy")
CORE = "cc"


def doc_index(position, new_lengths):
    ends = jnp.cumsum(new_lengths)
    return jnp.sum((ends[None, :] <= position[:, None]).astype(jnp.int32), axis=1)


def absorb_rows(nope_rows, w_uk):
    row_count = nope_rows.shape[0]
    heads_dev, nope_dim, latent_dim = w_uk.shape
    shaped = nope_rows.reshape(row_count, heads_dev, nope_dim)
    absorbed = jnp.einsum("thn,hnl->thl", shaped, w_uk, preferred_element_type=jnp.float32)
    return absorbed.astype(jnp.bfloat16)


def chip_index():
    return lax.axis_index("cz") * lax.axis_size("cy") + lax.axis_index("cy")


def shift_pairs(count, step):
    return [(i, (i - step) % count) for i in range(count)]


def gather_blocks(x, name):
    count = lax.axis_size(name)
    copies = jnp.broadcast_to(x[None], (count,) + x.shape)
    return lax.all_to_all(copies, name, 0, 0)


def spread_blocks(x, name):
    return lax.all_to_all(x, name, 0, 0)


def merge_parts(parts, heads_dev, value_dim):
    width = heads_dev * value_dim
    numer = parts[:, :, :width]
    peaks = parts[:, :, width : width + heads_dev]
    sums = parts[:, :, width + heads_dev :]
    peak = jnp.max(peaks, axis=0)
    shifted = jnp.where(jnp.isfinite(peak), peak, jnp.zeros_like(peak))
    scale = jnp.exp(peaks - shifted[None])
    count, rows = parts.shape[0], parts.shape[1]
    numer = numer.reshape(count, rows, heads_dev, value_dim) * scale[:, :, :, None]
    numer = jnp.sum(numer, axis=0).reshape(rows, width)
    total = jnp.sum(scale * sums, axis=0)
    return jnp.concatenate([numer, peak, total], axis=1)


def reduce_rows(x, heads_dev, value_dim):
    for name in ("cy", "cz"):
        count = lax.axis_size(name)
        blocks = x.reshape((count, x.shape[0] // count) + x.shape[1:])
        x = merge_parts(spread_blocks(blocks, name), heads_dev, value_dim)
    return x


def swap_cores(x):
    return lax.ppermute(x, CORE, [(0, 1), (1, 0)])


def body(q_nope, q_rope, w_uk, w_uv, cache, cache_scale, new_latent, cache_doc, new_lengths):
    tok_rows = q_nope.shape[0]
    heads_dev, nope_dim, latent_dim = w_uk.shape
    value_dim = w_uv.shape[2]
    rope_dim = q_rope.shape[1] // heads_dev
    cores = lax.axis_size(CORE)
    chips = 1
    for name in CHIP_PARTS:
        chips = chips * lax.axis_size(name)
    q_rows = tok_rows * chips
    my_chip = chip_index()
    my_core = lax.axis_index(CORE)
    other_core = 1 - my_core
    score_scale = (nope_dim + rope_dim) ** (-0.5)

    dequant = (cache.astype(jnp.float32) * cache_scale[:, None]).astype(jnp.bfloat16)
    own_keys = jnp.concatenate([dequant, new_latent], axis=0)
    other_keys = swap_cores(own_keys)
    other_doc = swap_cores(cache_doc)

    own_q = jnp.concatenate([q_nope, q_rope], axis=1)
    all_q = gather_blocks(own_q, "cz").reshape(-1, own_q.shape[1])
    all_q = gather_blocks(all_q, "cy").reshape(-1, own_q.shape[1])
    nope_width = heads_dev * nope_dim
    all_lat = absorb_rows(all_q[:, :nope_width], w_uk)
    all_rope = all_q[:, nope_width:]
    query = jnp.concatenate(
        [all_lat, all_rope.reshape(q_rows, heads_dev, rope_dim)],
        axis=2,
    )
    cache_len = cache.shape[0]
    block_len = cache_len // cache_doc.shape[0]
    row = jnp.arange(q_rows, dtype=jnp.int32)
    z_count = lax.axis_size("cz")
    row_chip = (row // tok_rows) % z_count * lax.axis_size("cy") + row // (tok_rows * z_count)
    query_pos = (row_chip * cores + my_core) * tok_rows + row % tok_rows
    query_doc = doc_index(query_pos, new_lengths)

    def key_meta(core, docs):
        new_pos = (my_chip * cores + core) * tok_rows + jnp.arange(tok_rows, dtype=jnp.int32)
        key_doc = jnp.concatenate([jnp.repeat(docs, block_len), doc_index(new_pos, new_lengths)])
        key_pos = jnp.concatenate([jnp.full((cache_len,), -1, dtype=jnp.int32), new_pos])
        return key_doc, key_pos

    own_doc, own_pos = key_meta(my_core, cache_doc)
    far_doc, far_pos = key_meta(other_core, other_doc)
    key_rows = jnp.concatenate([own_keys, other_keys], axis=0)
    key_doc = jnp.concatenate([own_doc, far_doc])
    key_pos = jnp.concatenate([own_pos, far_pos])
    allowed = (query_doc[:, None] == key_doc[None, :]) & (key_pos[None, :] <= query_pos[:, None])
    score = (
        jnp.einsum("qhl,kl->qhk", query, key_rows, preferred_element_type=jnp.float32) * score_scale
    )
    masked = jnp.where(allowed[:, None, :], score, -jnp.inf)
    local_max = jnp.max(masked, axis=2)
    shift = jnp.where(jnp.isfinite(local_max), local_max, jnp.zeros_like(local_max))
    weight = jnp.exp(masked - shift[:, :, None])
    totals = jnp.sum(weight, axis=2)
    weight_low = weight.astype(jnp.bfloat16)
    part_lat = jnp.einsum(
        "qhk,kl->qhl", weight_low, key_rows[:, :latent_dim], preferred_element_type=jnp.float32
    ).astype(jnp.bfloat16)
    numerator = jnp.einsum("qhl,hlv->qhv", part_lat, w_uv, preferred_element_type=jnp.float32)
    width = heads_dev * value_dim
    parts = jnp.concatenate([numerator.reshape(q_rows, width), local_max, totals], axis=1)
    merged = reduce_rows(parts, heads_dev, value_dim)
    own_numer = merged[:, :width].reshape(tok_rows, heads_dev, value_dim)
    own_total = merged[:, width + heads_dev :]
    result = own_numer / own_total[:, :, None]
    return result.astype(jnp.bfloat16).reshape(tok_rows, heads_dev * value_dim)


def solution(mesh):
    ctx_shape = (8, 4, 2)
    grid = np.asarray(mesh.devices).reshape(ctx_shape + (mesh.shape["wa"],))
    fine = Mesh(grid, CHIP_PARTS + (CORE, "wa"))
    rows = CHIP_PARTS + (CORE,)
    placed = (
        P(rows, "wa"),
        P(rows, "wa"),
        P("wa", None, None),
        P("wa", None, None),
        P(rows, None),
        P(rows),
        P(rows, None),
        P(rows),
        P(),
    )
    return jax.shard_map(
        body, mesh=fine, in_specs=placed, out_specs=P(rows, "wa"), check_vma=False
    )
```

```python
import jax
import jax.numpy as jnp
import numpy as np
from jax import lax
from jax.sharding import Mesh, PartitionSpec as P

CHIP_PARTS = ("cz", "cy")
CORE = "cc"


def doc_index(position, new_lengths):
    ends = jnp.cumsum(new_lengths)
    return jnp.sum((ends[None, :] <= position[:, None]).astype(jnp.int32), axis=1)


def absorb_rows(nope_rows, w_uk):
    row_count = nope_rows.shape[0]
    heads_dev, nope_dim, latent_dim = w_uk.shape
    shaped = nope_rows.reshape(row_count, heads_dev, nope_dim)
    absorbed = jnp.einsum("thn,hnl->thl", shaped, w_uk, preferred_element_type=jnp.float32)
    return absorbed.astype(jnp.bfloat16)


def chip_index():
    return lax.axis_index("cz") * lax.axis_size("cy") + lax.axis_index("cy")


def shift_pairs(count, step):
    return [(i, (i - step) % count) for i in range(count)]


def gather_blocks(x, name):
    count = 1
    for part in name:
        count = count * lax.axis_size(part)
    copies = jnp.broadcast_to(x[None], (count,) + x.shape)
    return lax.all_to_all(copies, name, 0, 0)


def spread_blocks(x, name):
    return lax.all_to_all(x, name, 0, 0)


def merge_parts(parts, heads_dev, value_dim):
    width = heads_dev * value_dim
    numer = parts[:, :, :width]
    peaks = parts[:, :, width : width + heads_dev]
    sums = parts[:, :, width + heads_dev :]
    peak = jnp.max(peaks, axis=0)
    shifted = jnp.where(jnp.isfinite(peak), peak, jnp.zeros_like(peak))
    scale = jnp.exp(peaks - shifted[None])
    count, rows = parts.shape[0], parts.shape[1]
    numer = numer.reshape(count, rows, heads_dev, value_dim) * scale[:, :, :, None]
    numer = jnp.sum(numer, axis=0).reshape(rows, width)
    total = jnp.sum(scale * sums, axis=0)
    return jnp.concatenate([numer, peak, total], axis=1)


def reduce_rows(x, heads_dev, value_dim):
    count = 1
    for name in CHIP_PARTS:
        count = count * lax.axis_size(name)
    blocks = x.reshape((count, x.shape[0] // count) + x.shape[1:])
    return merge_parts(spread_blocks(blocks, CHIP_PARTS), heads_dev, value_dim)


def swap_cores(x):
    return lax.ppermute(x, CORE, [(0, 1), (1, 0)])


def body(q_nope, q_rope, w_uk, w_uv, cache, cache_scale, new_latent, cache_doc, new_lengths):
    tok_rows = q_nope.shape[0]
    heads_dev, nope_dim, latent_dim = w_uk.shape
    value_dim = w_uv.shape[2]
    rope_dim = q_rope.shape[1] // heads_dev
    cores = lax.axis_size(CORE)
    chips = 1
    for name in CHIP_PARTS:
        chips = chips * lax.axis_size(name)
    q_rows = tok_rows * chips
    my_chip = chip_index()
    my_core = lax.axis_index(CORE)
    other_core = 1 - my_core
    score_scale = (nope_dim + rope_dim) ** (-0.5)

    dequant = (cache.astype(jnp.float32) * cache_scale[:, None]).astype(jnp.bfloat16)
    own_keys = jnp.concatenate([dequant, new_latent], axis=0)
    other_keys = swap_cores(own_keys)
    other_doc = swap_cores(cache_doc)

    own_q = jnp.concatenate([q_nope, q_rope], axis=1)
    all_q = gather_blocks(own_q, CHIP_PARTS).reshape(-1, own_q.shape[1])
    nope_width = heads_dev * nope_dim
    all_lat = absorb_rows(all_q[:, :nope_width], w_uk)
    all_rope = all_q[:, nope_width:]
    query = jnp.concatenate(
        [all_lat, all_rope.reshape(q_rows, heads_dev, rope_dim)],
        axis=2,
    )
    cache_len = cache.shape[0]
    block_len = cache_len // cache_doc.shape[0]
    row = jnp.arange(q_rows, dtype=jnp.int32)
    row_chip = row // tok_rows
    query_pos = (row_chip * cores + my_core) * tok_rows + row % tok_rows
    query_doc = doc_index(query_pos, new_lengths)

    def key_meta(core, docs):
        new_pos = (my_chip * cores + core) * tok_rows + jnp.arange(tok_rows, dtype=jnp.int32)
        key_doc = jnp.concatenate([jnp.repeat(docs, block_len), doc_index(new_pos, new_lengths)])
        key_pos = jnp.concatenate([jnp.full((cache_len,), -1, dtype=jnp.int32), new_pos])
        return key_doc, key_pos

    own_doc, own_pos = key_meta(my_core, cache_doc)
    far_doc, far_pos = key_meta(other_core, other_doc)
    key_rows = jnp.concatenate([own_keys, other_keys], axis=0)
    key_doc = jnp.concatenate([own_doc, far_doc])
    key_pos = jnp.concatenate([own_pos, far_pos])
    allowed = (query_doc[:, None] == key_doc[None, :]) & (key_pos[None, :] <= query_pos[:, None])
    score = (
        jnp.einsum("qhl,kl->qhk", query, key_rows, preferred_element_type=jnp.float32) * score_scale
    )
    masked = jnp.where(allowed[:, None, :], score, -jnp.inf)
    local_max = jnp.max(masked, axis=2)
    shift = jnp.where(jnp.isfinite(local_max), local_max, jnp.zeros_like(local_max))
    weight = jnp.exp(masked - shift[:, :, None])
    totals = jnp.sum(weight, axis=2)
    weight_low = weight.astype(jnp.bfloat16)
    part_lat = jnp.einsum(
        "qhk,kl->qhl", weight_low, key_rows[:, :latent_dim], preferred_element_type=jnp.float32
    ).astype(jnp.bfloat16)
    numerator = jnp.einsum("qhl,hlv->qhv", part_lat, w_uv, preferred_element_type=jnp.float32)
    width = heads_dev * value_dim
    parts = jnp.concatenate([numerator.reshape(q_rows, width), local_max, totals], axis=1)
    merged = reduce_rows(parts, heads_dev, value_dim)
    own_numer = merged[:, :width].reshape(tok_rows, heads_dev, value_dim)
    own_total = merged[:, width + heads_dev :]
    result = own_numer / own_total[:, :, None]
    return result.astype(jnp.bfloat16).reshape(tok_rows, heads_dev * value_dim)


def solution(mesh):
    ctx_shape = (8, 4, 2)
    grid = np.asarray(mesh.devices).reshape(ctx_shape + (mesh.shape["wa"],))
    fine = Mesh(grid, CHIP_PARTS + (CORE, "wa"))
    rows = CHIP_PARTS + (CORE,)
    placed = (
        P(rows, "wa"),
        P(rows, "wa"),
        P("wa", None, None),
        P("wa", None, None),
        P(rows, None),
        P(rows),
        P(rows, None),
        P(rows),
        P(),
    )
    return jax.shard_map(
        body, mesh=fine, in_specs=placed, out_specs=P(rows, "wa"), check_vma=False
    )
```

```python
import jax
import jax.numpy as jnp
import numpy as np
from jax import lax
from jax.sharding import Mesh, PartitionSpec as P
import functools
from jax.experimental import pallas as pl
from jax.experimental.pallas import tpu as pltpu

CHIP_PARTS = ("cz", "cy")
CORE = "cc"


def attend_kernel(scale, q_lat_ref, q_rope_ref, k_lat_ref, k_rope_ref, w_uv_ref, qdoc_ref, qpos_ref,
                  kdoc_ref, kpos_ref, numer_ref, peak_ref, sum_ref):
    k_lat = k_lat_ref[...]
    nt = (((1,), (1,)), ((), ()))
    score = lax.dot_general(q_lat_ref[0], k_lat, nt, preferred_element_type=jnp.float32)
    score = score + lax.dot_general(q_rope_ref[0], k_rope_ref[...], nt, preferred_element_type=jnp.float32)
    score = score * scale
    allowed = (qdoc_ref[...] == kdoc_ref[...]) & (kpos_ref[...] <= qpos_ref[...])
    masked = jnp.where(allowed, score, -jnp.inf)
    peak = jnp.max(masked, axis=1, keepdims=True)
    shift = jnp.where(peak > -jnp.inf, peak, 0.0)
    weight = jnp.where(allowed, jnp.exp(score - shift), 0.0)
    total = jnp.sum(weight, axis=1, keepdims=True)
    part = jnp.dot(weight.astype(jnp.bfloat16), k_lat, preferred_element_type=jnp.float32)
    numer = jnp.dot(part.astype(jnp.bfloat16), w_uv_ref[0], preferred_element_type=jnp.float32)
    numer_ref[0] = numer
    peak_ref[0] = peak
    sum_ref[0] = total


def attend(q_lat, q_rope, k_lat, k_rope, w_uv, qdoc, qpos, kdoc, kpos, scale, interpret=False):
    heads, rows, latent = q_lat.shape
    rope = q_rope.shape[2]
    keys = k_lat.shape[0]
    value = w_uv.shape[2]
    return pl.pallas_call(
        functools.partial(attend_kernel, scale),
        grid=(heads,),
        in_specs=[
            pl.BlockSpec((1, rows, latent), lambda h: (h, 0, 0)),
            pl.BlockSpec((1, rows, rope), lambda h: (h, 0, 0)),
            pl.BlockSpec((keys, latent), lambda h: (0, 0)),
            pl.BlockSpec((keys, rope), lambda h: (0, 0)),
            pl.BlockSpec((1, latent, value), lambda h: (h, 0, 0)),
            pl.BlockSpec((rows, 1), lambda h: (0, 0)),
            pl.BlockSpec((rows, 1), lambda h: (0, 0)),
            pl.BlockSpec((1, keys), lambda h: (0, 0)),
            pl.BlockSpec((1, keys), lambda h: (0, 0)),
        ],
        out_specs=[
            pl.BlockSpec((1, rows, value), lambda h: (h, 0, 0)),
            pl.BlockSpec((1, rows, 1), lambda h: (h, 0, 0)),
            pl.BlockSpec((1, rows, 1), lambda h: (h, 0, 0)),
        ],
        out_shape=[
            jax.ShapeDtypeStruct((heads, rows, value), jnp.float32),
            jax.ShapeDtypeStruct((heads, rows, 1), jnp.float32),
            jax.ShapeDtypeStruct((heads, rows, 1), jnp.float32),
        ],
        interpret=interpret,
    )(q_lat, q_rope, k_lat, k_rope, w_uv, qdoc, qpos, kdoc, kpos)


def doc_index(position, new_lengths):
    ends = jnp.cumsum(new_lengths)
    return jnp.sum((ends[None, :] <= position[:, None]).astype(jnp.int32), axis=1)


def absorb_rows(nope_rows, w_uk):
    row_count = nope_rows.shape[0]
    heads_dev, nope_dim, latent_dim = w_uk.shape
    shaped = nope_rows.reshape(row_count, heads_dev, nope_dim)
    absorbed = jnp.einsum("thn,hnl->thl", shaped, w_uk, preferred_element_type=jnp.float32)
    return absorbed.astype(jnp.bfloat16)


def chip_index():
    return lax.axis_index("cz") * lax.axis_size("cy") + lax.axis_index("cy")


def shift_pairs(count, step):
    return [(i, (i - step) % count) for i in range(count)]


def gather_blocks(x, name):
    count = lax.axis_size(name)
    copies = jnp.broadcast_to(x[None], (count,) + x.shape)
    return lax.all_to_all(copies, name, 0, 0)


def spread_blocks(x, name):
    return lax.all_to_all(x, name, 0, 0)


def merge_parts(parts, heads_dev, value_dim):
    width = heads_dev * value_dim
    numer = parts[:, :, :width]
    peaks = parts[:, :, width : width + heads_dev]
    sums = parts[:, :, width + heads_dev :]
    peak = jnp.max(peaks, axis=0)
    shifted = jnp.where(jnp.isfinite(peak), peak, jnp.zeros_like(peak))
    scale = jnp.exp(peaks - shifted[None])
    count, rows = parts.shape[0], parts.shape[1]
    numer = numer.reshape(count, rows, heads_dev, value_dim) * scale[:, :, :, None]
    numer = jnp.sum(numer, axis=0).reshape(rows, width)
    total = jnp.sum(scale * sums, axis=0)
    return jnp.concatenate([numer, peak, total], axis=1)


def reduce_rows(x, heads_dev, value_dim):
    for name in ("cy", "cz"):
        count = lax.axis_size(name)
        blocks = x.reshape((count, x.shape[0] // count) + x.shape[1:])
        x = merge_parts(spread_blocks(blocks, name), heads_dev, value_dim)
    return x


def swap_cores(x):
    return lax.ppermute(x, CORE, [(0, 1), (1, 0)])


def body(q_nope, q_rope, w_uk, w_uv, cache, cache_scale, new_latent, cache_doc, new_lengths):
    tok_rows = q_nope.shape[0]
    heads_dev, nope_dim, latent_dim = w_uk.shape
    value_dim = w_uv.shape[2]
    rope_dim = q_rope.shape[1] // heads_dev
    cores = lax.axis_size(CORE)
    chips = 1
    for name in CHIP_PARTS:
        chips = chips * lax.axis_size(name)
    q_rows = tok_rows * chips
    my_chip = chip_index()
    my_core = lax.axis_index(CORE)
    other_core = 1 - my_core
    score_scale = (nope_dim + rope_dim) ** (-0.5)

    dequant = (cache.astype(jnp.float32) * cache_scale[:, None]).astype(jnp.bfloat16)
    own_keys = jnp.concatenate([dequant, new_latent], axis=0)
    other_keys = swap_cores(own_keys)
    other_doc = swap_cores(cache_doc)

    own_q = jnp.concatenate([q_nope, q_rope], axis=1)
    all_q = gather_blocks(own_q, "cz").reshape(-1, own_q.shape[1])
    all_q = gather_blocks(all_q, "cy").reshape(-1, own_q.shape[1])
    nope_width = heads_dev * nope_dim
    head_q = all_q[:, :nope_width].reshape(q_rows, heads_dev, nope_dim)
    q_lat = jnp.einsum("thn,hnl->htl", head_q, w_uk, preferred_element_type=jnp.float32)
    q_lat = q_lat.astype(jnp.bfloat16)
    q_rot = all_q[:, nope_width:].reshape(q_rows, heads_dev, rope_dim).transpose(1, 0, 2)
    cache_len = cache.shape[0]
    block_len = cache_len // cache_doc.shape[0]
    row = jnp.arange(q_rows, dtype=jnp.int32)
    z_count = lax.axis_size("cz")
    row_chip = (row // tok_rows) % z_count * lax.axis_size("cy") + row // (tok_rows * z_count)
    query_pos = (row_chip * cores + my_core) * tok_rows + row % tok_rows
    query_doc = doc_index(query_pos, new_lengths)

    def key_meta(core, docs):
        new_pos = (my_chip * cores + core) * tok_rows + jnp.arange(tok_rows, dtype=jnp.int32)
        key_doc = jnp.concatenate([jnp.repeat(docs, block_len), doc_index(new_pos, new_lengths)])
        key_pos = jnp.concatenate([jnp.full((cache_len,), -1, dtype=jnp.int32), new_pos])
        return key_doc, key_pos

    own_doc, own_pos = key_meta(my_core, cache_doc)
    far_doc, far_pos = key_meta(other_core, other_doc)
    key_rows = jnp.concatenate([own_keys, other_keys], axis=0)
    key_doc = jnp.concatenate([own_doc, far_doc])
    key_pos = jnp.concatenate([own_pos, far_pos])
    numer, peak, total = attend(
        q_lat, q_rot, key_rows[:, :latent_dim], key_rows[:, latent_dim:], w_uv,
        query_doc[:, None], query_pos[:, None], key_doc[None, :], key_pos[None, :], score_scale,
    )
    numerator = numer.transpose(1, 0, 2)
    local_max = peak[:, :, 0].T
    totals = total[:, :, 0].T
    width = heads_dev * value_dim
    parts = jnp.concatenate([numerator.reshape(q_rows, width), local_max, totals], axis=1)
    merged = reduce_rows(parts, heads_dev, value_dim)
    own_numer = merged[:, :width].reshape(tok_rows, heads_dev, value_dim)
    own_total = merged[:, width + heads_dev :]
    result = own_numer / own_total[:, :, None]
    return result.astype(jnp.bfloat16).reshape(tok_rows, heads_dev * value_dim)


def solution(mesh):
    ctx_shape = (8, 4, 2)
    grid = np.asarray(mesh.devices).reshape(ctx_shape + (mesh.shape["wa"],))
    fine = Mesh(grid, CHIP_PARTS + (CORE, "wa"))
    rows = CHIP_PARTS + (CORE,)
    placed = (
        P(rows, "wa"),
        P(rows, "wa"),
        P("wa", None, None),
        P("wa", None, None),
        P(rows, None),
        P(rows),
        P(rows, None),
        P(rows),
        P(),
    )
    return jax.shard_map(
        body, mesh=fine, in_specs=placed, out_specs=P(rows, "wa"), check_vma=False
    )
```

```python
import jax
import jax.numpy as jnp
import numpy as np
from jax import lax
from jax.sharding import Mesh, PartitionSpec as P
import functools
from jax.experimental import pallas as pl
from jax.experimental.pallas import tpu as pltpu

CHIP_PARTS = ("cz", "cy")
PAIR = "zp"
CORE = "cc"


def attend_kernel(scale, q_lat_ref, q_rope_ref, k_lat_ref, k_rope_ref, w_uv_ref, qdoc_ref, qpos_ref,
                  kdoc_ref, kpos_ref, numer_ref, peak_ref, sum_ref):
    k_lat = k_lat_ref[...]
    nt = (((1,), (1,)), ((), ()))
    score = lax.dot_general(q_lat_ref[0], k_lat, nt, preferred_element_type=jnp.float32)
    score = score + lax.dot_general(q_rope_ref[0], k_rope_ref[...], nt, preferred_element_type=jnp.float32)
    score = score * scale
    allowed = (qdoc_ref[...] == kdoc_ref[...]) & (kpos_ref[...] <= qpos_ref[...])
    masked = jnp.where(allowed, score, -jnp.inf)
    peak = jnp.max(masked, axis=1, keepdims=True)
    shift = jnp.where(peak > -jnp.inf, peak, 0.0)
    weight = jnp.where(allowed, jnp.exp(score - shift), 0.0)
    total = jnp.sum(weight, axis=1, keepdims=True)
    part = jnp.dot(weight.astype(jnp.bfloat16), k_lat, preferred_element_type=jnp.float32)
    numer = jnp.dot(part.astype(jnp.bfloat16), w_uv_ref[0], preferred_element_type=jnp.float32)
    numer_ref[0] = numer
    peak_ref[0] = peak
    sum_ref[0] = total


def attend(q_lat, q_rope, k_lat, k_rope, w_uv, qdoc, qpos, kdoc, kpos, scale, interpret=False):
    heads, rows, latent = q_lat.shape
    rope = q_rope.shape[2]
    keys = k_lat.shape[0]
    value = w_uv.shape[2]
    return pl.pallas_call(
        functools.partial(attend_kernel, scale),
        grid=(heads,),
        in_specs=[
            pl.BlockSpec((1, rows, latent), lambda h: (h, 0, 0)),
            pl.BlockSpec((1, rows, rope), lambda h: (h, 0, 0)),
            pl.BlockSpec((keys, latent), lambda h: (0, 0)),
            pl.BlockSpec((keys, rope), lambda h: (0, 0)),
            pl.BlockSpec((1, latent, value), lambda h: (h, 0, 0)),
            pl.BlockSpec((rows, 1), lambda h: (0, 0)),
            pl.BlockSpec((rows, 1), lambda h: (0, 0)),
            pl.BlockSpec((1, keys), lambda h: (0, 0)),
            pl.BlockSpec((1, keys), lambda h: (0, 0)),
        ],
        out_specs=[
            pl.BlockSpec((1, rows, value), lambda h: (h, 0, 0)),
            pl.BlockSpec((1, rows, 1), lambda h: (h, 0, 0)),
            pl.BlockSpec((1, rows, 1), lambda h: (h, 0, 0)),
        ],
        out_shape=[
            jax.ShapeDtypeStruct((heads, rows, value), jnp.float32),
            jax.ShapeDtypeStruct((heads, rows, 1), jnp.float32),
            jax.ShapeDtypeStruct((heads, rows, 1), jnp.float32),
        ],
        interpret=interpret,
    )(q_lat, q_rope, k_lat, k_rope, w_uv, qdoc, qpos, kdoc, kpos)


def doc_index(position, new_lengths):
    ends = jnp.cumsum(new_lengths)
    return jnp.sum((ends[None, :] <= position[:, None]).astype(jnp.int32), axis=1)


def absorb_rows(nope_rows, w_uk):
    row_count = nope_rows.shape[0]
    heads_dev, nope_dim, latent_dim = w_uk.shape
    shaped = nope_rows.reshape(row_count, heads_dev, nope_dim)
    absorbed = jnp.einsum("thn,hnl->thl", shaped, w_uk, preferred_element_type=jnp.float32)
    return absorbed.astype(jnp.bfloat16)


def swap_pair(x):
    return lax.ppermute(x, PAIR, [(0, 1), (1, 0)])


def shift_pairs(count, step):
    return [(i, (i - step) % count) for i in range(count)]


def gather_blocks(x, name):
    count = lax.axis_size(name)
    copies = jnp.broadcast_to(x[None], (count,) + x.shape)
    return lax.all_to_all(copies, name, 0, 0)


def spread_blocks(x, name):
    return lax.all_to_all(x, name, 0, 0)


def merge_parts(parts, heads_dev, value_dim):
    width = heads_dev * value_dim
    numer = parts[:, :, :width]
    peaks = parts[:, :, width : width + heads_dev]
    sums = parts[:, :, width + heads_dev :]
    peak = jnp.max(peaks, axis=0)
    shifted = jnp.where(jnp.isfinite(peak), peak, jnp.zeros_like(peak))
    scale = jnp.exp(peaks - shifted[None])
    count, rows = parts.shape[0], parts.shape[1]
    numer = numer.reshape(count, rows, heads_dev, value_dim) * scale[:, :, :, None]
    numer = jnp.sum(numer, axis=0).reshape(rows, width)
    total = jnp.sum(scale * sums, axis=0)
    return jnp.concatenate([numer, peak, total], axis=1)


def reduce_rows(x, heads_dev, value_dim):
    for name in ("cy", "cz"):
        count = lax.axis_size(name)
        blocks = x.reshape((count, x.shape[0] // count) + x.shape[1:])
        x = merge_parts(spread_blocks(blocks, name), heads_dev, value_dim)
    return x


def swap_cores(x):
    return lax.ppermute(x, CORE, [(0, 1), (1, 0)])


def body(q_nope, q_rope, w_uk, w_uv, cache, cache_scale, new_latent, cache_doc, new_lengths):
    tok_rows = q_nope.shape[0]
    heads_dev, nope_dim, latent_dim = w_uk.shape
    value_dim = w_uv.shape[2]
    rope_dim = q_rope.shape[1] // heads_dev
    z_count = lax.axis_size("cz")
    y_count = lax.axis_size("cy")
    pairs = lax.axis_size(PAIR)
    cores = lax.axis_size(CORE)
    q_rows = tok_rows * z_count * y_count
    my_z = lax.axis_index("cz")
    my_y = lax.axis_index("cy")
    my_pair = lax.axis_index(PAIR)
    my_core = lax.axis_index(CORE)
    score_scale = (nope_dim + rope_dim) ** (-0.5)

    def owner(z, pair, y, core):
        return ((z * pairs + pair) * y_count + y) * cores + core

    dequant = (cache.astype(jnp.float32) * cache_scale[:, None]).astype(jnp.bfloat16)
    own_keys = jnp.concatenate([dequant, new_latent], axis=0)
    chip_keys = jnp.concatenate([own_keys, swap_cores(own_keys)], axis=0)
    chip_doc = jnp.concatenate([cache_doc, swap_cores(cache_doc)])
    key_rows = jnp.concatenate([chip_keys, swap_pair(chip_keys)], axis=0)
    pool_doc = jnp.concatenate([chip_doc, swap_pair(chip_doc)])

    own_q = jnp.concatenate([q_nope, q_rope], axis=1)
    all_q = gather_blocks(own_q, "cz").reshape(-1, own_q.shape[1])
    all_q = gather_blocks(all_q, "cy").reshape(-1, own_q.shape[1])
    nope_width = heads_dev * nope_dim
    head_q = all_q[:, :nope_width].reshape(q_rows, heads_dev, nope_dim)
    q_lat = jnp.einsum("thn,hnl->htl", head_q, w_uk, preferred_element_type=jnp.float32)
    q_lat = q_lat.astype(jnp.bfloat16)
    q_rot = all_q[:, nope_width:].reshape(q_rows, heads_dev, rope_dim).transpose(1, 0, 2)
    cache_len = cache.shape[0]
    block_len = cache_len // cache_doc.shape[0]
    row = jnp.arange(q_rows, dtype=jnp.int32)
    row_z = (row // tok_rows) % z_count
    row_y = row // (tok_rows * z_count)
    query_pos = owner(row_z, my_pair, row_y, my_core) * tok_rows + row % tok_rows
    query_doc = doc_index(query_pos, new_lengths)

    metas = []
    for pair, core in ((my_pair, my_core), (my_pair, 1 - my_core), (1 - my_pair, my_core), (1 - my_pair, 1 - my_core)):
        new_pos = owner(my_z, pair, my_y, core) * tok_rows + jnp.arange(tok_rows, dtype=jnp.int32)
        metas.append((doc_index(new_pos, new_lengths), new_pos))
    slot_docs = pool_doc.reshape(len(metas), -1)
    key_doc = jnp.concatenate(
        [jnp.concatenate([jnp.repeat(slot_docs[i], block_len), metas[i][0]]) for i in range(len(metas))]
    )
    key_pos = jnp.concatenate(
        [jnp.concatenate([jnp.full((cache_len,), -1, dtype=jnp.int32), metas[i][1]]) for i in range(len(metas))]
    )
    numer, peak, total = attend(
        q_lat, q_rot, key_rows[:, :latent_dim], key_rows[:, latent_dim:], w_uv,
        query_doc[:, None], query_pos[:, None], key_doc[None, :], key_pos[None, :], score_scale,
    )
    numerator = numer.transpose(1, 0, 2)
    local_max = peak[:, :, 0].T
    totals = total[:, :, 0].T
    width = heads_dev * value_dim
    parts = jnp.concatenate([numerator.reshape(q_rows, width), local_max, totals], axis=1)
    merged = reduce_rows(parts, heads_dev, value_dim)
    own_numer = merged[:, :width].reshape(tok_rows, heads_dev, value_dim)
    own_total = merged[:, width + heads_dev :]
    result = own_numer / own_total[:, :, None]
    return result.astype(jnp.bfloat16).reshape(tok_rows, heads_dev * value_dim)


def solution(mesh):
    ctx_shape = (4, 2, 4, 2)
    grid = np.asarray(mesh.devices).reshape(ctx_shape + (mesh.shape["wa"],))
    fine = Mesh(grid, ("cz", PAIR, "cy", CORE, "wa"))
    rows = ("cz", PAIR, "cy", CORE)
    placed = (
        P(rows, "wa"),
        P(rows, "wa"),
        P("wa", None, None),
        P("wa", None, None),
        P(rows, None),
        P(rows),
        P(rows, None),
        P(rows),
        P(),
    )
    return jax.shard_map(
        body, mesh=fine, in_specs=placed, out_specs=P(rows, "wa"), check_vma=False
    )
```

```python
import jax
import jax.numpy as jnp
import numpy as np
from jax import lax
from jax.sharding import Mesh, PartitionSpec as P
import functools
from jax.experimental import pallas as pl
from jax.experimental.pallas import tpu as pltpu

CHIP_PARTS = ("cz", "cy")
PAIR = "zp"
CORE = "cc"


def attend_kernel(scale, q_lat_ref, q_rope_ref, k_lat_ref, k_rope_ref, w_uv_ref, qdoc_ref, qpos_ref,
                  kdoc_ref, kpos_ref, numer_ref, peak_ref, sum_ref):
    k_lat = k_lat_ref[...]
    nt = (((1,), (1,)), ((), ()))
    score = lax.dot_general(q_lat_ref[0], k_lat, nt, preferred_element_type=jnp.float32)
    score = score + lax.dot_general(q_rope_ref[0], k_rope_ref[...], nt, preferred_element_type=jnp.float32)
    score = score * scale
    allowed = (qdoc_ref[...] == kdoc_ref[...]) & (kpos_ref[...] <= qpos_ref[...])
    masked = jnp.where(allowed, score, -jnp.inf)
    peak = jnp.max(masked, axis=1, keepdims=True)
    shift = jnp.where(peak > -jnp.inf, peak, 0.0)
    weight = jnp.where(allowed, jnp.exp(score - shift), 0.0)
    total = jnp.sum(weight, axis=1, keepdims=True)
    part = jnp.dot(weight.astype(jnp.bfloat16), k_lat, preferred_element_type=jnp.float32)
    numer = jnp.dot(part.astype(jnp.bfloat16), w_uv_ref[0], preferred_element_type=jnp.float32)
    numer_ref[0] = numer
    peak_ref[0] = peak
    sum_ref[0] = total


def attend(q_lat, q_rope, k_lat, k_rope, w_uv, qdoc, qpos, kdoc, kpos, scale, interpret=False):
    heads, rows, latent = q_lat.shape
    rope = q_rope.shape[2]
    keys = k_lat.shape[0]
    value = w_uv.shape[2]
    return pl.pallas_call(
        functools.partial(attend_kernel, scale),
        grid=(heads,),
        in_specs=[
            pl.BlockSpec((1, rows, latent), lambda h: (h, 0, 0)),
            pl.BlockSpec((1, rows, rope), lambda h: (h, 0, 0)),
            pl.BlockSpec((keys, latent), lambda h: (0, 0)),
            pl.BlockSpec((keys, rope), lambda h: (0, 0)),
            pl.BlockSpec((1, latent, value), lambda h: (h, 0, 0)),
            pl.BlockSpec((rows, 1), lambda h: (0, 0)),
            pl.BlockSpec((rows, 1), lambda h: (0, 0)),
            pl.BlockSpec((1, keys), lambda h: (0, 0)),
            pl.BlockSpec((1, keys), lambda h: (0, 0)),
        ],
        out_specs=[
            pl.BlockSpec((1, rows, value), lambda h: (h, 0, 0)),
            pl.BlockSpec((1, rows, 1), lambda h: (h, 0, 0)),
            pl.BlockSpec((1, rows, 1), lambda h: (h, 0, 0)),
        ],
        out_shape=[
            jax.ShapeDtypeStruct((heads, rows, value), jnp.float32),
            jax.ShapeDtypeStruct((heads, rows, 1), jnp.float32),
            jax.ShapeDtypeStruct((heads, rows, 1), jnp.float32),
        ],
        interpret=interpret,
    )(q_lat, q_rope, k_lat, k_rope, w_uv, qdoc, qpos, kdoc, kpos)


def doc_index(position, new_lengths):
    ends = jnp.cumsum(new_lengths)
    return jnp.sum((ends[None, :] <= position[:, None]).astype(jnp.int32), axis=1)


def absorb_rows(nope_rows, w_uk):
    row_count = nope_rows.shape[0]
    heads_dev, nope_dim, latent_dim = w_uk.shape
    shaped = nope_rows.reshape(row_count, heads_dev, nope_dim)
    absorbed = jnp.einsum("thn,hnl->thl", shaped, w_uk, preferred_element_type=jnp.float32)
    return absorbed.astype(jnp.bfloat16)


def swap_pair(x):
    return lax.ppermute(x, PAIR, [(0, 1), (1, 0)])


def swap_diag(x):
    return lax.ppermute(x, (PAIR, CORE), [(0, 3), (1, 2), (2, 1), (3, 0)])


def shift_pairs(count, step):
    return [(i, (i - step) % count) for i in range(count)]


def gather_blocks(x, name):
    count = lax.axis_size(name)
    copies = jnp.broadcast_to(x[None], (count,) + x.shape)
    return lax.all_to_all(copies, name, 0, 0)


def spread_blocks(x, name):
    return lax.all_to_all(x, name, 0, 0)


def merge_parts(parts, heads_dev, value_dim):
    width = heads_dev * value_dim
    numer = parts[:, :, :width]
    peaks = parts[:, :, width : width + heads_dev]
    sums = parts[:, :, width + heads_dev :]
    peak = jnp.max(peaks, axis=0)
    shifted = jnp.where(jnp.isfinite(peak), peak, jnp.zeros_like(peak))
    scale = jnp.exp(peaks - shifted[None])
    count, rows = parts.shape[0], parts.shape[1]
    numer = numer.reshape(count, rows, heads_dev, value_dim) * scale[:, :, :, None]
    numer = jnp.sum(numer, axis=0).reshape(rows, width)
    total = jnp.sum(scale * sums, axis=0)
    return jnp.concatenate([numer, peak, total], axis=1)


def reduce_rows(x, heads_dev, value_dim):
    for name in ("cy", "cz"):
        count = lax.axis_size(name)
        blocks = x.reshape((count, x.shape[0] // count) + x.shape[1:])
        x = merge_parts(spread_blocks(blocks, name), heads_dev, value_dim)
    return x


def swap_cores(x):
    return lax.ppermute(x, CORE, [(0, 1), (1, 0)])


def body(q_nope, q_rope, w_uk, w_uv, cache, cache_scale, new_latent, cache_doc, new_lengths):
    tok_rows = q_nope.shape[0]
    heads_dev, nope_dim, latent_dim = w_uk.shape
    value_dim = w_uv.shape[2]
    rope_dim = q_rope.shape[1] // heads_dev
    z_count = lax.axis_size("cz")
    y_count = lax.axis_size("cy")
    pairs = lax.axis_size(PAIR)
    cores = lax.axis_size(CORE)
    q_rows = tok_rows * z_count * y_count
    my_z = lax.axis_index("cz")
    my_y = lax.axis_index("cy")
    my_pair = lax.axis_index(PAIR)
    my_core = lax.axis_index(CORE)
    score_scale = (nope_dim + rope_dim) ** (-0.5)

    def owner(z, pair, y, core):
        return ((z * pairs + pair) * y_count + y) * cores + core

    dequant = (cache.astype(jnp.float32) * cache_scale[:, None]).astype(jnp.bfloat16)
    own_keys = jnp.concatenate([dequant, new_latent], axis=0)
    key_rows = jnp.concatenate(
        [own_keys, swap_cores(own_keys), swap_pair(own_keys), swap_diag(own_keys)], axis=0
    )
    pool_doc = jnp.concatenate(
        [cache_doc, swap_cores(cache_doc), swap_pair(cache_doc), swap_diag(cache_doc)]
    )

    own_q = jnp.concatenate([q_nope, q_rope], axis=1)
    all_q = gather_blocks(own_q, "cz").reshape(-1, own_q.shape[1])
    all_q = gather_blocks(all_q, "cy").reshape(-1, own_q.shape[1])
    nope_width = heads_dev * nope_dim
    head_q = all_q[:, :nope_width].reshape(q_rows, heads_dev, nope_dim)
    q_lat = jnp.einsum("thn,hnl->htl", head_q, w_uk, preferred_element_type=jnp.float32)
    q_lat = q_lat.astype(jnp.bfloat16)
    q_rot = all_q[:, nope_width:].reshape(q_rows, heads_dev, rope_dim).transpose(1, 0, 2)
    cache_len = cache.shape[0]
    block_len = cache_len // cache_doc.shape[0]
    row = jnp.arange(q_rows, dtype=jnp.int32)
    row_z = (row // tok_rows) % z_count
    row_y = row // (tok_rows * z_count)
    query_pos = owner(row_z, my_pair, row_y, my_core) * tok_rows + row % tok_rows
    query_doc = doc_index(query_pos, new_lengths)

    metas = []
    for pair, core in ((my_pair, my_core), (my_pair, 1 - my_core), (1 - my_pair, my_core), (1 - my_pair, 1 - my_core)):
        new_pos = owner(my_z, pair, my_y, core) * tok_rows + jnp.arange(tok_rows, dtype=jnp.int32)
        metas.append((doc_index(new_pos, new_lengths), new_pos))
    slot_docs = pool_doc.reshape(len(metas), -1)
    key_doc = jnp.concatenate(
        [jnp.concatenate([jnp.repeat(slot_docs[i], block_len), metas[i][0]]) for i in range(len(metas))]
    )
    key_pos = jnp.concatenate(
        [jnp.concatenate([jnp.full((cache_len,), -1, dtype=jnp.int32), metas[i][1]]) for i in range(len(metas))]
    )
    numer, peak, total = attend(
        q_lat, q_rot, key_rows[:, :latent_dim], key_rows[:, latent_dim:], w_uv,
        query_doc[:, None], query_pos[:, None], key_doc[None, :], key_pos[None, :], score_scale,
    )
    numerator = numer.transpose(1, 0, 2)
    local_max = peak[:, :, 0].T
    totals = total[:, :, 0].T
    width = heads_dev * value_dim
    parts = jnp.concatenate([numerator.reshape(q_rows, width), local_max, totals], axis=1)
    merged = reduce_rows(parts, heads_dev, value_dim)
    own_numer = merged[:, :width].reshape(tok_rows, heads_dev, value_dim)
    own_total = merged[:, width + heads_dev :]
    result = own_numer / own_total[:, :, None]
    return result.astype(jnp.bfloat16).reshape(tok_rows, heads_dev * value_dim)


def solution(mesh):
    ctx_shape = (4, 2, 4, 2)
    grid = np.asarray(mesh.devices).reshape(ctx_shape + (mesh.shape["wa"],))
    fine = Mesh(grid, ("cz", PAIR, "cy", CORE, "wa"))
    rows = ("cz", PAIR, "cy", CORE)
    placed = (
        P(rows, "wa"),
        P(rows, "wa"),
        P("wa", None, None),
        P("wa", None, None),
        P(rows, None),
        P(rows),
        P(rows, None),
        P(rows),
        P(),
    )
    return jax.shard_map(
        body, mesh=fine, in_specs=placed, out_specs=P(rows, "wa"), check_vma=False
    )
```

```python
import jax
import jax.numpy as jnp
import numpy as np
from jax import lax
from jax.sharding import Mesh, PartitionSpec as P
import functools
from jax.experimental import pallas as pl
from jax.experimental.pallas import tpu as pltpu

CHIP_PARTS = ("cz", "cy")
CORE = "cc"


def attend_kernel(scale, latent, q_nope_ref, w_uk_ref, q_rope_ref, keys_ref, w_uv_ref, qdoc_ref,
                  qpos_ref, kdoc_ref, kpos_ref, numer_ref, peak_ref, sum_ref):
    q_lat = jnp.dot(q_nope_ref[...], w_uk_ref[0], preferred_element_type=jnp.float32)
    q_lat = q_lat.astype(jnp.bfloat16)
    k_lat = keys_ref[:, :latent]
    nt = (((1,), (1,)), ((), ()))
    score = lax.dot_general(q_lat, k_lat, nt, preferred_element_type=jnp.float32)
    score = score + lax.dot_general(
        q_rope_ref[0], keys_ref[:, latent:], nt, preferred_element_type=jnp.float32
    )
    score = score * scale
    allowed = (qdoc_ref[...] == kdoc_ref[...]) & (kpos_ref[...] <= qpos_ref[...])
    masked = jnp.where(allowed, score, -jnp.inf)
    peak = jnp.max(masked, axis=1, keepdims=True)
    shift = jnp.where(peak > -jnp.inf, peak, 0.0)
    weight = jnp.where(allowed, jnp.exp(score - shift), 0.0)
    total = jnp.sum(weight, axis=1, keepdims=True)
    part = jnp.dot(weight.astype(jnp.bfloat16), k_lat, preferred_element_type=jnp.float32)
    numer = jnp.dot(part.astype(jnp.bfloat16), w_uv_ref[0], preferred_element_type=jnp.float32)
    numer_ref[...] = numer
    peak_ref[0] = peak
    sum_ref[0] = total


def attend(all_q, w_uk, q_rope, keys, w_uv, qdoc, qpos, kdoc, kpos, scale, interpret=False):
    heads, nope, latent = w_uk.shape
    rows = all_q.shape[0]
    rope = q_rope.shape[2]
    key_count, width = keys.shape
    value = w_uv.shape[2]
    return pl.pallas_call(
        functools.partial(attend_kernel, scale, latent),
        grid=(heads,),
        in_specs=[
            pl.BlockSpec((rows, nope), lambda h: (0, h)),
            pl.BlockSpec((1, nope, latent), lambda h: (h, 0, 0)),
            pl.BlockSpec((1, rows, rope), lambda h: (h, 0, 0)),
            pl.BlockSpec((key_count, width), lambda h: (0, 0)),
            pl.BlockSpec((1, latent, value), lambda h: (h, 0, 0)),
            pl.BlockSpec((rows, 1), lambda h: (0, 0)),
            pl.BlockSpec((rows, 1), lambda h: (0, 0)),
            pl.BlockSpec((1, key_count), lambda h: (0, 0)),
            pl.BlockSpec((1, key_count), lambda h: (0, 0)),
        ],
        out_specs=[
            pl.BlockSpec((rows, value), lambda h: (0, h)),
            pl.BlockSpec((1, rows, 1), lambda h: (h, 0, 0)),
            pl.BlockSpec((1, rows, 1), lambda h: (h, 0, 0)),
        ],
        out_shape=[
            jax.ShapeDtypeStruct((rows, heads * value), jnp.float32),
            jax.ShapeDtypeStruct((heads, rows, 1), jnp.float32),
            jax.ShapeDtypeStruct((heads, rows, 1), jnp.float32),
        ],
        interpret=interpret,
    )(all_q, w_uk, q_rope, keys, w_uv, qdoc, qpos, kdoc, kpos)


def doc_index(position, new_lengths):
    ends = jnp.cumsum(new_lengths)
    return jnp.sum((ends[None, :] <= position[:, None]).astype(jnp.int32), axis=1)


def absorb_rows(nope_rows, w_uk):
    row_count = nope_rows.shape[0]
    heads_dev, nope_dim, latent_dim = w_uk.shape
    shaped = nope_rows.reshape(row_count, heads_dev, nope_dim)
    absorbed = jnp.einsum("thn,hnl->thl", shaped, w_uk, preferred_element_type=jnp.float32)
    return absorbed.astype(jnp.bfloat16)


def chip_index():
    return lax.axis_index("cz") * lax.axis_size("cy") + lax.axis_index("cy")


def shift_pairs(count, step):
    return [(i, (i - step) % count) for i in range(count)]


def gather_blocks(x, name):
    count = lax.axis_size(name)
    copies = jnp.broadcast_to(x[None], (count,) + x.shape)
    return lax.all_to_all(copies, name, 0, 0)


def spread_blocks(x, name):
    return lax.all_to_all(x, name, 0, 0)


def merge_parts(parts, heads_dev, value_dim):
    width = heads_dev * value_dim
    numer = parts[:, :, :width]
    peaks = parts[:, :, width : width + heads_dev]
    sums = parts[:, :, width + heads_dev :]
    peak = jnp.max(peaks, axis=0)
    shifted = jnp.where(jnp.isfinite(peak), peak, jnp.zeros_like(peak))
    scale = jnp.exp(peaks - shifted[None])
    count, rows = parts.shape[0], parts.shape[1]
    numer = numer.reshape(count, rows, heads_dev, value_dim) * scale[:, :, :, None]
    numer = jnp.sum(numer, axis=0).reshape(rows, width)
    total = jnp.sum(scale * sums, axis=0)
    return jnp.concatenate([numer, peak, total], axis=1)


def reduce_rows(x, heads_dev, value_dim):
    for name in ("cy", "cz"):
        count = lax.axis_size(name)
        blocks = x.reshape((count, x.shape[0] // count) + x.shape[1:])
        x = merge_parts(spread_blocks(blocks, name), heads_dev, value_dim)
    return x


def swap_cores(x):
    return lax.ppermute(x, CORE, [(0, 1), (1, 0)])


def body(q_nope, q_rope, w_uk, w_uv, cache, cache_scale, new_latent, cache_doc, new_lengths):
    tok_rows = q_nope.shape[0]
    heads_dev, nope_dim, latent_dim = w_uk.shape
    value_dim = w_uv.shape[2]
    rope_dim = q_rope.shape[1] // heads_dev
    cores = lax.axis_size(CORE)
    chips = 1
    for name in CHIP_PARTS:
        chips = chips * lax.axis_size(name)
    q_rows = tok_rows * chips
    my_chip = chip_index()
    my_core = lax.axis_index(CORE)
    other_core = 1 - my_core
    score_scale = (nope_dim + rope_dim) ** (-0.5)

    dequant = (cache.astype(jnp.float32) * cache_scale[:, None]).astype(jnp.bfloat16)
    own_keys = jnp.concatenate([dequant, new_latent], axis=0)
    other_keys = swap_cores(own_keys)
    other_doc = swap_cores(cache_doc)

    own_q = jnp.concatenate([q_nope, q_rope], axis=1)
    all_q = gather_blocks(own_q, "cz").reshape(-1, own_q.shape[1])
    all_q = gather_blocks(all_q, "cy").reshape(-1, own_q.shape[1])
    nope_width = heads_dev * nope_dim
    q_rot = all_q[:, nope_width:].reshape(q_rows, heads_dev, rope_dim).transpose(1, 0, 2)
    cache_len = cache.shape[0]
    block_len = cache_len // cache_doc.shape[0]
    row = jnp.arange(q_rows, dtype=jnp.int32)
    z_count = lax.axis_size("cz")
    row_chip = (row // tok_rows) % z_count * lax.axis_size("cy") + row // (tok_rows * z_count)
    query_pos = (row_chip * cores + my_core) * tok_rows + row % tok_rows
    query_doc = doc_index(query_pos, new_lengths)

    def key_meta(core, docs):
        new_pos = (my_chip * cores + core) * tok_rows + jnp.arange(tok_rows, dtype=jnp.int32)
        key_doc = jnp.concatenate([jnp.repeat(docs, block_len), doc_index(new_pos, new_lengths)])
        key_pos = jnp.concatenate([jnp.full((cache_len,), -1, dtype=jnp.int32), new_pos])
        return key_doc, key_pos

    own_doc, own_pos = key_meta(my_core, cache_doc)
    far_doc, far_pos = key_meta(other_core, other_doc)
    key_rows = jnp.concatenate([own_keys, other_keys], axis=0)
    key_doc = jnp.concatenate([own_doc, far_doc])
    key_pos = jnp.concatenate([own_pos, far_pos])
    numer, peak, total = attend(
        all_q, w_uk, q_rot, key_rows, w_uv,
        query_doc[:, None], query_pos[:, None], key_doc[None, :], key_pos[None, :], score_scale,
    )
    local_max = peak[:, :, 0].T
    totals = total[:, :, 0].T
    width = heads_dev * value_dim
    parts = jnp.concatenate([numer, local_max, totals], axis=1)
    merged = reduce_rows(parts, heads_dev, value_dim)
    own_numer = merged[:, :width].reshape(tok_rows, heads_dev, value_dim)
    own_total = merged[:, width + heads_dev :]
    result = own_numer / own_total[:, :, None]
    return result.astype(jnp.bfloat16).reshape(tok_rows, heads_dev * value_dim)


def solution(mesh):
    ctx_shape = (8, 4, 2)
    grid = np.asarray(mesh.devices).reshape(ctx_shape + (mesh.shape["wa"],))
    fine = Mesh(grid, CHIP_PARTS + (CORE, "wa"))
    rows = CHIP_PARTS + (CORE,)
    placed = (
        P(rows, "wa"),
        P(rows, "wa"),
        P("wa", None, None),
        P("wa", None, None),
        P(rows, None),
        P(rows),
        P(rows, None),
        P(rows),
        P(),
    )
    return jax.shard_map(
        body, mesh=fine, in_specs=placed, out_specs=P(rows, "wa"), check_vma=False
    )
```

```python
import jax
import jax.numpy as jnp
import numpy as np
from jax import lax
from jax.sharding import Mesh, PartitionSpec as P
import functools
from jax.experimental import pallas as pl
from jax.experimental.pallas import tpu as pltpu

CHIP_PARTS = ("cz", "cy")
CORE = "cc"


def attend_kernel(scale, latent, q_nope_ref, w_uk_ref, q_rope_ref, keys_ref, w_uv_ref, qdoc_ref,
                  qpos_ref, kdoc_ref, kpos_ref, numer_ref, peak_ref, sum_ref, bias_ref):
    @pl.when(pl.program_id(0) == 0)
    def _():
        allowed = (qdoc_ref[...] == kdoc_ref[...]) & (kpos_ref[...] <= qpos_ref[...])
        bias_ref[...] = jnp.where(allowed, 0.0, -jnp.inf)

    q_lat = jnp.dot(q_nope_ref[...], w_uk_ref[0], preferred_element_type=jnp.float32)
    q_lat = q_lat.astype(jnp.bfloat16)
    k_lat = keys_ref[:, :latent]
    nt = (((1,), (1,)), ((), ()))
    score = lax.dot_general(q_lat, k_lat, nt, preferred_element_type=jnp.float32)
    score = score + lax.dot_general(
        q_rope_ref[0], keys_ref[:, latent:], nt, preferred_element_type=jnp.float32
    )
    masked = score * scale + bias_ref[...]
    peak = jnp.max(masked, axis=1, keepdims=True)
    shift = jnp.where(peak > -jnp.inf, peak, 0.0)
    weight = jnp.exp(masked - shift)
    total = jnp.sum(weight, axis=1, keepdims=True)
    part = jnp.dot(weight.astype(jnp.bfloat16), k_lat, preferred_element_type=jnp.float32)
    numer = jnp.dot(part.astype(jnp.bfloat16), w_uv_ref[0], preferred_element_type=jnp.float32)
    numer_ref[...] = numer
    peak_ref[0] = peak
    sum_ref[0] = total


def attend(all_q, w_uk, q_rope, keys, w_uv, qdoc, qpos, kdoc, kpos, scale, interpret=False):
    heads, nope, latent = w_uk.shape
    rows = all_q.shape[0]
    rope = q_rope.shape[2]
    key_count, width = keys.shape
    value = w_uv.shape[2]
    return pl.pallas_call(
        functools.partial(attend_kernel, scale, latent),
        grid=(heads,),
        in_specs=[
            pl.BlockSpec((rows, nope), lambda h: (0, h)),
            pl.BlockSpec((1, nope, latent), lambda h: (h, 0, 0)),
            pl.BlockSpec((1, rows, rope), lambda h: (h, 0, 0)),
            pl.BlockSpec((key_count, width), lambda h: (0, 0)),
            pl.BlockSpec((1, latent, value), lambda h: (h, 0, 0)),
            pl.BlockSpec((rows, 1), lambda h: (0, 0)),
            pl.BlockSpec((rows, 1), lambda h: (0, 0)),
            pl.BlockSpec((1, key_count), lambda h: (0, 0)),
            pl.BlockSpec((1, key_count), lambda h: (0, 0)),
        ],
        out_specs=[
            pl.BlockSpec((rows, value), lambda h: (0, h)),
            pl.BlockSpec((1, rows, 1), lambda h: (h, 0, 0)),
            pl.BlockSpec((1, rows, 1), lambda h: (h, 0, 0)),
        ],
        out_shape=[
            jax.ShapeDtypeStruct((rows, heads * value), jnp.float32),
            jax.ShapeDtypeStruct((heads, rows, 1), jnp.float32),
            jax.ShapeDtypeStruct((heads, rows, 1), jnp.float32),
        ],
        scratch_shapes=[pltpu.VMEM((rows, key_count), jnp.float32)],
        interpret=interpret,
    )(all_q, w_uk, q_rope, keys, w_uv, qdoc, qpos, kdoc, kpos)


def doc_index(position, new_lengths):
    ends = jnp.cumsum(new_lengths)
    return jnp.sum((ends[None, :] <= position[:, None]).astype(jnp.int32), axis=1)


def absorb_rows(nope_rows, w_uk):
    row_count = nope_rows.shape[0]
    heads_dev, nope_dim, latent_dim = w_uk.shape
    shaped = nope_rows.reshape(row_count, heads_dev, nope_dim)
    absorbed = jnp.einsum("thn,hnl->thl", shaped, w_uk, preferred_element_type=jnp.float32)
    return absorbed.astype(jnp.bfloat16)


def chip_index():
    return lax.axis_index("cz") * lax.axis_size("cy") + lax.axis_index("cy")


def shift_pairs(count, step):
    return [(i, (i - step) % count) for i in range(count)]


def gather_blocks(x, name):
    count = lax.axis_size(name)
    copies = jnp.broadcast_to(x[None], (count,) + x.shape)
    return lax.all_to_all(copies, name, 0, 0)


def spread_blocks(x, name):
    return lax.all_to_all(x, name, 0, 0)


def merge_parts(parts, heads_dev, value_dim):
    width = heads_dev * value_dim
    numer = parts[:, :, :width]
    peaks = parts[:, :, width : width + heads_dev]
    sums = parts[:, :, width + heads_dev :]
    peak = jnp.max(peaks, axis=0)
    shifted = jnp.where(jnp.isfinite(peak), peak, jnp.zeros_like(peak))
    scale = jnp.exp(peaks - shifted[None])
    count, rows = parts.shape[0], parts.shape[1]
    numer = numer.reshape(count, rows, heads_dev, value_dim) * scale[:, :, :, None]
    numer = jnp.sum(numer, axis=0).reshape(rows, width)
    total = jnp.sum(scale * sums, axis=0)
    return jnp.concatenate([numer, peak, total], axis=1)


def reduce_rows(x, heads_dev, value_dim):
    for name in ("cy", "cz"):
        count = lax.axis_size(name)
        blocks = x.reshape((count, x.shape[0] // count) + x.shape[1:])
        x = merge_parts(spread_blocks(blocks, name), heads_dev, value_dim)
    return x


def swap_cores(x):
    return lax.ppermute(x, CORE, [(0, 1), (1, 0)])


def body(q_nope, q_rope, w_uk, w_uv, cache, cache_scale, new_latent, cache_doc, new_lengths):
    tok_rows = q_nope.shape[0]
    heads_dev, nope_dim, latent_dim = w_uk.shape
    value_dim = w_uv.shape[2]
    rope_dim = q_rope.shape[1] // heads_dev
    cores = lax.axis_size(CORE)
    chips = 1
    for name in CHIP_PARTS:
        chips = chips * lax.axis_size(name)
    q_rows = tok_rows * chips
    my_chip = chip_index()
    my_core = lax.axis_index(CORE)
    other_core = 1 - my_core
    score_scale = (nope_dim + rope_dim) ** (-0.5)

    dequant = (cache.astype(jnp.float32) * cache_scale[:, None]).astype(jnp.bfloat16)
    own_keys = jnp.concatenate([dequant, new_latent], axis=0)
    other_keys = swap_cores(own_keys)
    other_doc = swap_cores(cache_doc)

    own_q = jnp.concatenate([q_nope, q_rope], axis=1)
    all_q = gather_blocks(own_q, "cz").reshape(-1, own_q.shape[1])
    all_q = gather_blocks(all_q, "cy").reshape(-1, own_q.shape[1])
    nope_width = heads_dev * nope_dim
    q_rot = all_q[:, nope_width:].reshape(q_rows, heads_dev, rope_dim).transpose(1, 0, 2)
    cache_len = cache.shape[0]
    block_len = cache_len // cache_doc.shape[0]
    row = jnp.arange(q_rows, dtype=jnp.int32)
    z_count = lax.axis_size("cz")
    row_chip = (row // tok_rows) % z_count * lax.axis_size("cy") + row // (tok_rows * z_count)
    query_pos = (row_chip * cores + my_core) * tok_rows + row % tok_rows
    query_doc = doc_index(query_pos, new_lengths)

    def key_meta(core, docs):
        new_pos = (my_chip * cores + core) * tok_rows + jnp.arange(tok_rows, dtype=jnp.int32)
        key_doc = jnp.concatenate([jnp.repeat(docs, block_len), doc_index(new_pos, new_lengths)])
        key_pos = jnp.concatenate([jnp.full((cache_len,), -1, dtype=jnp.int32), new_pos])
        return key_doc, key_pos

    own_doc, own_pos = key_meta(my_core, cache_doc)
    far_doc, far_pos = key_meta(other_core, other_doc)
    key_rows = jnp.concatenate([own_keys, other_keys], axis=0)
    key_doc = jnp.concatenate([own_doc, far_doc])
    key_pos = jnp.concatenate([own_pos, far_pos])
    numer, peak, total = attend(
        all_q, w_uk, q_rot, key_rows, w_uv,
        query_doc[:, None], query_pos[:, None], key_doc[None, :], key_pos[None, :], score_scale,
    )
    local_max = peak[:, :, 0].T
    totals = total[:, :, 0].T
    width = heads_dev * value_dim
    parts = jnp.concatenate([numer, local_max, totals], axis=1)
    merged = reduce_rows(parts, heads_dev, value_dim)
    own_numer = merged[:, :width].reshape(tok_rows, heads_dev, value_dim)
    own_total = merged[:, width + heads_dev :]
    result = own_numer / own_total[:, :, None]
    return result.astype(jnp.bfloat16).reshape(tok_rows, heads_dev * value_dim)


def solution(mesh):
    ctx_shape = (8, 4, 2)
    grid = np.asarray(mesh.devices).reshape(ctx_shape + (mesh.shape["wa"],))
    fine = Mesh(grid, CHIP_PARTS + (CORE, "wa"))
    rows = CHIP_PARTS + (CORE,)
    placed = (
        P(rows, "wa"),
        P(rows, "wa"),
        P("wa", None, None),
        P("wa", None, None),
        P(rows, None),
        P(rows),
        P(rows, None),
        P(rows),
        P(),
    )
    return jax.shard_map(
        body, mesh=fine, in_specs=placed, out_specs=P(rows, "wa"), check_vma=False
    )
```

```python
import jax
import jax.numpy as jnp
import numpy as np
from jax import lax
from jax.sharding import Mesh, PartitionSpec as P
import functools
from jax.experimental import pallas as pl
from jax.experimental.pallas import tpu as pltpu

CHIP_PARTS = ("cz", "cy")
CORE = "cc"


def attend_kernel(scale, latent, q_nope_ref, w_uk_ref, q_rope_ref, keys_ref, w_uv_ref, qdoc_ref,
                  qpos_ref, kdoc_ref, kpos_ref, numer_ref, stats_ref, bias_ref):
    head = pl.program_id(0)
    heads = pl.num_programs(0)

    @pl.when(head == 0)
    def _():
        allowed = (qdoc_ref[...] == kdoc_ref[...]) & (kpos_ref[...] <= qpos_ref[...])
        bias_ref[...] = jnp.where(allowed, 0.0, -jnp.inf)
        stats_ref[...] = jnp.zeros(stats_ref.shape, jnp.float32)

    q_lat = jnp.dot(q_nope_ref[...], w_uk_ref[0], preferred_element_type=jnp.float32)
    q_lat = q_lat.astype(jnp.bfloat16)
    k_lat = keys_ref[:, :latent]
    nt = (((1,), (1,)), ((), ()))
    score = lax.dot_general(q_lat, k_lat, nt, preferred_element_type=jnp.float32)
    score = score + lax.dot_general(
        q_rope_ref[0], keys_ref[:, latent:], nt, preferred_element_type=jnp.float32
    )
    masked = score * scale + bias_ref[...]
    peak = jnp.max(masked, axis=1, keepdims=True)
    shift = jnp.where(peak > -jnp.inf, peak, 0.0)
    weight = jnp.exp(masked - shift)
    total = jnp.sum(weight, axis=1, keepdims=True)
    part = jnp.dot(weight.astype(jnp.bfloat16), k_lat, preferred_element_type=jnp.float32)
    numer = jnp.dot(part.astype(jnp.bfloat16), w_uv_ref[0], preferred_element_type=jnp.float32)
    numer_ref[...] = numer
    lane = lax.broadcasted_iota(jnp.int32, stats_ref.shape, 1)
    stats = jnp.where(lane == head, peak, stats_ref[...])
    stats_ref[...] = jnp.where(lane == heads + head, total, stats)


def attend(all_q, w_uk, q_rope, keys, w_uv, qdoc, qpos, kdoc, kpos, scale, interpret=False):
    heads, nope, latent = w_uk.shape
    rows = all_q.shape[0]
    rope = q_rope.shape[2]
    key_count, width = keys.shape
    value = w_uv.shape[2]
    return pl.pallas_call(
        functools.partial(attend_kernel, scale, latent),
        grid=(heads,),
        in_specs=[
            pl.BlockSpec((rows, nope), lambda h: (0, h)),
            pl.BlockSpec((1, nope, latent), lambda h: (h, 0, 0)),
            pl.BlockSpec((1, rows, rope), lambda h: (h, 0, 0)),
            pl.BlockSpec((key_count, width), lambda h: (0, 0)),
            pl.BlockSpec((1, latent, value), lambda h: (h, 0, 0)),
            pl.BlockSpec((rows, 1), lambda h: (0, 0)),
            pl.BlockSpec((rows, 1), lambda h: (0, 0)),
            pl.BlockSpec((1, key_count), lambda h: (0, 0)),
            pl.BlockSpec((1, key_count), lambda h: (0, 0)),
        ],
        out_specs=[
            pl.BlockSpec((rows, value), lambda h: (0, h)),
            pl.BlockSpec((rows, 128), lambda h: (0, 0)),
        ],
        out_shape=[
            jax.ShapeDtypeStruct((rows, heads * value), jnp.float32),
            jax.ShapeDtypeStruct((rows, 128), jnp.float32),
        ],
        scratch_shapes=[pltpu.VMEM((rows, key_count), jnp.float32)],
        interpret=interpret,
    )(all_q, w_uk, q_rope, keys, w_uv, qdoc, qpos, kdoc, kpos)


def doc_index(position, new_lengths):
    ends = jnp.cumsum(new_lengths)
    return jnp.sum((ends[None, :] <= position[:, None]).astype(jnp.int32), axis=1)


def absorb_rows(nope_rows, w_uk):
    row_count = nope_rows.shape[0]
    heads_dev, nope_dim, latent_dim = w_uk.shape
    shaped = nope_rows.reshape(row_count, heads_dev, nope_dim)
    absorbed = jnp.einsum("thn,hnl->thl", shaped, w_uk, preferred_element_type=jnp.float32)
    return absorbed.astype(jnp.bfloat16)


def chip_index():
    return lax.axis_index("cz") * lax.axis_size("cy") + lax.axis_index("cy")


def shift_pairs(count, step):
    return [(i, (i - step) % count) for i in range(count)]


def gather_blocks(x, name):
    count = lax.axis_size(name)
    copies = jnp.broadcast_to(x[None], (count,) + x.shape)
    return lax.all_to_all(copies, name, 0, 0)


def spread_blocks(x, name):
    return lax.all_to_all(x, name, 0, 0)


def merge_parts(parts, heads_dev, value_dim):
    width = heads_dev * value_dim
    numer = parts[:, :, :width]
    peaks = parts[:, :, width : width + heads_dev]
    sums = parts[:, :, width + heads_dev :]
    peak = jnp.max(peaks, axis=0)
    shifted = jnp.where(jnp.isfinite(peak), peak, jnp.zeros_like(peak))
    scale = jnp.exp(peaks - shifted[None])
    count, rows = parts.shape[0], parts.shape[1]
    numer = numer.reshape(count, rows, heads_dev, value_dim) * scale[:, :, :, None]
    numer = jnp.sum(numer, axis=0).reshape(rows, width)
    total = jnp.sum(scale * sums, axis=0)
    return jnp.concatenate([numer, peak, total], axis=1)


def reduce_rows(x, heads_dev, value_dim):
    for name in ("cy", "cz"):
        count = lax.axis_size(name)
        blocks = x.reshape((count, x.shape[0] // count) + x.shape[1:])
        x = merge_parts(spread_blocks(blocks, name), heads_dev, value_dim)
    return x


def swap_cores(x):
    return lax.ppermute(x, CORE, [(0, 1), (1, 0)])


def body(q_nope, q_rope, w_uk, w_uv, cache, cache_scale, new_latent, cache_doc, new_lengths):
    tok_rows = q_nope.shape[0]
    heads_dev, nope_dim, latent_dim = w_uk.shape
    value_dim = w_uv.shape[2]
    rope_dim = q_rope.shape[1] // heads_dev
    cores = lax.axis_size(CORE)
    chips = 1
    for name in CHIP_PARTS:
        chips = chips * lax.axis_size(name)
    q_rows = tok_rows * chips
    my_chip = chip_index()
    my_core = lax.axis_index(CORE)
    other_core = 1 - my_core
    score_scale = (nope_dim + rope_dim) ** (-0.5)

    dequant = (cache.astype(jnp.float32) * cache_scale[:, None]).astype(jnp.bfloat16)
    own_keys = jnp.concatenate([dequant, new_latent], axis=0)
    other_keys = swap_cores(own_keys)
    other_doc = swap_cores(cache_doc)

    own_q = jnp.concatenate([q_nope, q_rope], axis=1)
    all_q = gather_blocks(own_q, "cz").reshape(-1, own_q.shape[1])
    all_q = gather_blocks(all_q, "cy").reshape(-1, own_q.shape[1])
    nope_width = heads_dev * nope_dim
    q_rot = all_q[:, nope_width:].reshape(q_rows, heads_dev, rope_dim).transpose(1, 0, 2)
    cache_len = cache.shape[0]
    block_len = cache_len // cache_doc.shape[0]
    row = jnp.arange(q_rows, dtype=jnp.int32)
    z_count = lax.axis_size("cz")
    row_chip = (row // tok_rows) % z_count * lax.axis_size("cy") + row // (tok_rows * z_count)
    query_pos = (row_chip * cores + my_core) * tok_rows + row % tok_rows
    query_doc = doc_index(query_pos, new_lengths)

    def key_meta(core, docs):
        new_pos = (my_chip * cores + core) * tok_rows + jnp.arange(tok_rows, dtype=jnp.int32)
        key_doc = jnp.concatenate([jnp.repeat(docs, block_len), doc_index(new_pos, new_lengths)])
        key_pos = jnp.concatenate([jnp.full((cache_len,), -1, dtype=jnp.int32), new_pos])
        return key_doc, key_pos

    own_doc, own_pos = key_meta(my_core, cache_doc)
    far_doc, far_pos = key_meta(other_core, other_doc)
    key_rows = jnp.concatenate([own_keys, other_keys], axis=0)
    key_doc = jnp.concatenate([own_doc, far_doc])
    key_pos = jnp.concatenate([own_pos, far_pos])
    numer, stats = attend(
        all_q, w_uk, q_rot, key_rows, w_uv,
        query_doc[:, None], query_pos[:, None], key_doc[None, :], key_pos[None, :], score_scale,
    )
    width = heads_dev * value_dim
    parts = jnp.concatenate([numer, stats[:, : 2 * heads_dev]], axis=1)
    merged = reduce_rows(parts, heads_dev, value_dim)
    own_numer = merged[:, :width].reshape(tok_rows, heads_dev, value_dim)
    own_total = merged[:, width + heads_dev :]
    result = own_numer / own_total[:, :, None]
    return result.astype(jnp.bfloat16).reshape(tok_rows, heads_dev * value_dim)


def solution(mesh):
    ctx_shape = (8, 4, 2)
    grid = np.asarray(mesh.devices).reshape(ctx_shape + (mesh.shape["wa"],))
    fine = Mesh(grid, CHIP_PARTS + (CORE, "wa"))
    rows = CHIP_PARTS + (CORE,)
    placed = (
        P(rows, "wa"),
        P(rows, "wa"),
        P("wa", None, None),
        P("wa", None, None),
        P(rows, None),
        P(rows),
        P(rows, None),
        P(rows),
        P(),
    )
    return jax.shard_map(
        body, mesh=fine, in_specs=placed, out_specs=P(rows, "wa"), check_vma=False
    )
```

```python
import jax
import jax.numpy as jnp
import numpy as np
from jax import lax
from jax.sharding import Mesh, PartitionSpec as P
import functools
from jax.experimental import pallas as pl
from jax.experimental.pallas import tpu as pltpu

CHIP_PARTS = ("cz", "cy")
CORE = "cc"


def attend_kernel(scale, latent, q_nope_ref, w_uk_ref, q_rope_ref, keys_ref, w_uv_ref, qdoc_ref,
                  qpos_ref, kdoc_ref, kpos_ref, numer_ref, stats_ref, bias_ref):
    head = pl.program_id(0)
    heads = pl.num_programs(0)

    @pl.when(head == 0)
    def _():
        allowed = (qdoc_ref[...] == kdoc_ref[...]) & (kpos_ref[...] <= qpos_ref[...])
        bias_ref[...] = jnp.where(allowed, 0.0, -jnp.inf)
        stats_ref[...] = jnp.zeros(stats_ref.shape, jnp.float32)

    q_lat = jnp.dot(q_nope_ref[...], w_uk_ref[0], preferred_element_type=jnp.float32)
    q_lat = q_lat.astype(jnp.bfloat16)
    k_lat = keys_ref[:, :latent]
    nt = (((1,), (1,)), ((), ()))
    score = lax.dot_general(q_lat, k_lat, nt, preferred_element_type=jnp.float32)
    score = score + lax.dot_general(
        q_rope_ref[0], keys_ref[:, latent:], nt, preferred_element_type=jnp.float32
    )
    masked = score * scale + bias_ref[...]
    peak = jnp.max(masked, axis=1, keepdims=True)
    shift = jnp.where(peak > -jnp.inf, peak, 0.0)
    weight = jnp.exp(masked - shift)
    total = jnp.sum(weight, axis=1, keepdims=True)
    part = jnp.dot(weight.astype(jnp.bfloat16), k_lat, preferred_element_type=jnp.float32)
    numer = jnp.dot(part.astype(jnp.bfloat16), w_uv_ref[0], preferred_element_type=jnp.float32)
    numer_ref[...] = numer
    lane = lax.broadcasted_iota(jnp.int32, stats_ref.shape, 1)
    stats = jnp.where(lane == head, peak, stats_ref[...])
    stats_ref[...] = jnp.where(lane == heads + head, total, stats)


def attend(all_q, w_uk, q_rope, keys, w_uv, qdoc, qpos, kdoc, kpos, scale, interpret=False):
    heads, nope, latent = w_uk.shape
    rows = all_q.shape[0]
    rope = q_rope.shape[2]
    key_count, width = keys.shape
    value = w_uv.shape[2]
    return pl.pallas_call(
        functools.partial(attend_kernel, scale, latent),
        grid=(heads,),
        in_specs=[
            pl.BlockSpec((rows, nope), lambda h: (0, h)),
            pl.BlockSpec((1, nope, latent), lambda h: (h, 0, 0)),
            pl.BlockSpec((1, rows, rope), lambda h: (h, 0, 0)),
            pl.BlockSpec((key_count, width), lambda h: (0, 0)),
            pl.BlockSpec((1, latent, value), lambda h: (h, 0, 0)),
            pl.BlockSpec((rows, 1), lambda h: (0, 0)),
            pl.BlockSpec((rows, 1), lambda h: (0, 0)),
            pl.BlockSpec((1, key_count), lambda h: (0, 0)),
            pl.BlockSpec((1, key_count), lambda h: (0, 0)),
        ],
        out_specs=[
            pl.BlockSpec((rows, value), lambda h: (0, h)),
            pl.BlockSpec((rows, 128), lambda h: (0, 0)),
        ],
        out_shape=[
            jax.ShapeDtypeStruct((rows, heads * value), jnp.float32),
            jax.ShapeDtypeStruct((rows, 128), jnp.float32),
        ],
        scratch_shapes=[pltpu.VMEM((rows, key_count), jnp.float32)],
        interpret=interpret,
    )(all_q, w_uk, q_rope, keys, w_uv, qdoc, qpos, kdoc, kpos)


def doc_index(position, new_lengths):
    ends = jnp.cumsum(new_lengths)
    return jnp.sum((ends[None, :] <= position[:, None]).astype(jnp.int32), axis=1)


def absorb_rows(nope_rows, w_uk):
    row_count = nope_rows.shape[0]
    heads_dev, nope_dim, latent_dim = w_uk.shape
    shaped = nope_rows.reshape(row_count, heads_dev, nope_dim)
    absorbed = jnp.einsum("thn,hnl->thl", shaped, w_uk, preferred_element_type=jnp.float32)
    return absorbed.astype(jnp.bfloat16)


def chip_index():
    return lax.axis_index("cz") * lax.axis_size("cy") + lax.axis_index("cy")


def shift_pairs(count, step):
    return [(i, (i - step) % count) for i in range(count)]


def gather_blocks(x, name):
    count = lax.axis_size(name)
    copies = jnp.broadcast_to(x[None], (count,) + x.shape)
    return lax.all_to_all(copies, name, 0, 0)


def spread_blocks(x, name):
    return lax.all_to_all(x, name, 0, 0)


def merge_parts(parts, heads_dev, value_dim):
    width = heads_dev * value_dim
    numer = parts[:, :, :width]
    peaks = parts[:, :, width : width + heads_dev]
    sums = parts[:, :, width + heads_dev :]
    peak = jnp.max(peaks, axis=0)
    shifted = jnp.where(jnp.isfinite(peak), peak, jnp.zeros_like(peak))
    scale = jnp.exp(peaks - shifted[None])
    count, rows = parts.shape[0], parts.shape[1]
    numer = numer.reshape(count, rows, heads_dev, value_dim) * scale[:, :, :, None]
    numer = jnp.sum(numer, axis=0).reshape(rows, width)
    total = jnp.sum(scale * sums, axis=0)
    return jnp.concatenate([numer, peak, total], axis=1)


def reduce_rows(x, heads_dev, value_dim):
    for name in ("cz", "cy"):
        count = lax.axis_size(name)
        blocks = x.reshape((count, x.shape[0] // count) + x.shape[1:])
        x = merge_parts(spread_blocks(blocks, name), heads_dev, value_dim)
    return x


def swap_cores(x):
    return lax.ppermute(x, CORE, [(0, 1), (1, 0)])


def body(q_nope, q_rope, w_uk, w_uv, cache, cache_scale, new_latent, cache_doc, new_lengths):
    tok_rows = q_nope.shape[0]
    heads_dev, nope_dim, latent_dim = w_uk.shape
    value_dim = w_uv.shape[2]
    rope_dim = q_rope.shape[1] // heads_dev
    cores = lax.axis_size(CORE)
    chips = 1
    for name in CHIP_PARTS:
        chips = chips * lax.axis_size(name)
    q_rows = tok_rows * chips
    my_chip = chip_index()
    my_core = lax.axis_index(CORE)
    other_core = 1 - my_core
    score_scale = (nope_dim + rope_dim) ** (-0.5)

    dequant = (cache.astype(jnp.float32) * cache_scale[:, None]).astype(jnp.bfloat16)
    own_keys = jnp.concatenate([dequant, new_latent], axis=0)
    other_keys = swap_cores(own_keys)
    other_doc = swap_cores(cache_doc)

    own_q = jnp.concatenate([q_nope, q_rope], axis=1)
    all_q = gather_blocks(own_q, "cy").reshape(-1, own_q.shape[1])
    all_q = gather_blocks(all_q, "cz").reshape(-1, own_q.shape[1])
    nope_width = heads_dev * nope_dim
    q_rot = all_q[:, nope_width:].reshape(q_rows, heads_dev, rope_dim).transpose(1, 0, 2)
    cache_len = cache.shape[0]
    block_len = cache_len // cache_doc.shape[0]
    row = jnp.arange(q_rows, dtype=jnp.int32)
    row_chip = row // tok_rows
    query_pos = (row_chip * cores + my_core) * tok_rows + row % tok_rows
    query_doc = doc_index(query_pos, new_lengths)

    def key_meta(core, docs):
        new_pos = (my_chip * cores + core) * tok_rows + jnp.arange(tok_rows, dtype=jnp.int32)
        key_doc = jnp.concatenate([jnp.repeat(docs, block_len), doc_index(new_pos, new_lengths)])
        key_pos = jnp.concatenate([jnp.full((cache_len,), -1, dtype=jnp.int32), new_pos])
        return key_doc, key_pos

    own_doc, own_pos = key_meta(my_core, cache_doc)
    far_doc, far_pos = key_meta(other_core, other_doc)
    key_rows = jnp.concatenate([own_keys, other_keys], axis=0)
    key_doc = jnp.concatenate([own_doc, far_doc])
    key_pos = jnp.concatenate([own_pos, far_pos])
    numer, stats = attend(
        all_q, w_uk, q_rot, key_rows, w_uv,
        query_doc[:, None], query_pos[:, None], key_doc[None, :], key_pos[None, :], score_scale,
    )
    width = heads_dev * value_dim
    parts = jnp.concatenate([numer, stats[:, : 2 * heads_dev]], axis=1)
    merged = reduce_rows(parts, heads_dev, value_dim)
    own_numer = merged[:, :width].reshape(tok_rows, heads_dev, value_dim)
    own_total = merged[:, width + heads_dev :]
    result = own_numer / own_total[:, :, None]
    return result.astype(jnp.bfloat16).reshape(tok_rows, heads_dev * value_dim)


def solution(mesh):
    ctx_shape = (8, 4, 2)
    grid = np.asarray(mesh.devices).reshape(ctx_shape + (mesh.shape["wa"],))
    fine = Mesh(grid, CHIP_PARTS + (CORE, "wa"))
    rows = CHIP_PARTS + (CORE,)
    placed = (
        P(rows, "wa"),
        P(rows, "wa"),
        P("wa", None, None),
        P("wa", None, None),
        P(rows, None),
        P(rows),
        P(rows, None),
        P(rows),
        P(),
    )
    return jax.shard_map(
        body, mesh=fine, in_specs=placed, out_specs=P(rows, "wa"), check_vma=False
    )
```

```python
import jax
import jax.numpy as jnp
import numpy as np
from jax import lax
from jax.sharding import Mesh, PartitionSpec as P
import functools
from jax.experimental import pallas as pl
from jax.experimental.pallas import tpu as pltpu

CHIP_PARTS = ("cz", "cy")
CORE = "cc"


def attend_kernel(scale, latent, q_nope_ref, w_uk_ref, q_rope_ref, keys_ref, keys_t_ref, w_uv_ref, qdoc_ref,
                  qpos_ref, kdoc_ref, kpos_ref, numer_ref, stats_ref, bias_ref):
    head = pl.program_id(0)
    heads = pl.num_programs(0)

    @pl.when(head == 0)
    def _():
        allowed = (qdoc_ref[...] == kdoc_ref[...]) & (kpos_ref[...] <= qpos_ref[...])
        bias_ref[...] = jnp.where(allowed, 0.0, -jnp.inf)
        stats_ref[...] = jnp.zeros(stats_ref.shape, jnp.float32)

    q_lat = jnp.dot(q_nope_ref[...], w_uk_ref[0], preferred_element_type=jnp.float32)
    q_lat = q_lat.astype(jnp.bfloat16)
    k_lat = keys_ref[:, :latent]
    score = jnp.dot(q_lat, keys_t_ref[:latent, :], preferred_element_type=jnp.float32)
    score = score + jnp.dot(q_rope_ref[0], keys_t_ref[latent:, :], preferred_element_type=jnp.float32)
    masked = score * scale + bias_ref[...]
    peak = jnp.max(masked, axis=1, keepdims=True)
    shift = jnp.where(peak > -jnp.inf, peak, 0.0)
    weight = jnp.exp(masked - shift)
    total = jnp.sum(weight, axis=1, keepdims=True)
    part = jnp.dot(weight.astype(jnp.bfloat16), k_lat, preferred_element_type=jnp.float32)
    numer = jnp.dot(part.astype(jnp.bfloat16), w_uv_ref[0], preferred_element_type=jnp.float32)
    numer_ref[...] = numer
    lane = lax.broadcasted_iota(jnp.int32, stats_ref.shape, 1)
    stats = jnp.where(lane == head, peak, stats_ref[...])
    stats_ref[...] = jnp.where(lane == heads + head, total, stats)


def attend(all_q, w_uk, q_rope, keys, w_uv, qdoc, qpos, kdoc, kpos, scale, interpret=False):
    heads, nope, latent = w_uk.shape
    rows = all_q.shape[0]
    rope = q_rope.shape[2]
    key_count, width = keys.shape
    value = w_uv.shape[2]
    return pl.pallas_call(
        functools.partial(attend_kernel, scale, latent),
        grid=(heads,),
        in_specs=[
            pl.BlockSpec((rows, nope), lambda h: (0, h)),
            pl.BlockSpec((1, nope, latent), lambda h: (h, 0, 0)),
            pl.BlockSpec((1, rows, rope), lambda h: (h, 0, 0)),
            pl.BlockSpec((key_count, width), lambda h: (0, 0)),
            pl.BlockSpec((width, key_count), lambda h: (0, 0)),
            pl.BlockSpec((1, latent, value), lambda h: (h, 0, 0)),
            pl.BlockSpec((rows, 1), lambda h: (0, 0)),
            pl.BlockSpec((rows, 1), lambda h: (0, 0)),
            pl.BlockSpec((1, key_count), lambda h: (0, 0)),
            pl.BlockSpec((1, key_count), lambda h: (0, 0)),
        ],
        out_specs=[
            pl.BlockSpec((rows, value), lambda h: (0, h)),
            pl.BlockSpec((rows, 128), lambda h: (0, 0)),
        ],
        out_shape=[
            jax.ShapeDtypeStruct((rows, heads * value), jnp.float32),
            jax.ShapeDtypeStruct((rows, 128), jnp.float32),
        ],
        scratch_shapes=[pltpu.VMEM((rows, key_count), jnp.float32)],
        interpret=interpret,
    )(all_q, w_uk, q_rope, keys, keys.T, w_uv, qdoc, qpos, kdoc, kpos)


def doc_index(position, new_lengths):
    ends = jnp.cumsum(new_lengths)
    return jnp.sum((ends[None, :] <= position[:, None]).astype(jnp.int32), axis=1)


def absorb_rows(nope_rows, w_uk):
    row_count = nope_rows.shape[0]
    heads_dev, nope_dim, latent_dim = w_uk.shape
    shaped = nope_rows.reshape(row_count, heads_dev, nope_dim)
    absorbed = jnp.einsum("thn,hnl->thl", shaped, w_uk, preferred_element_type=jnp.float32)
    return absorbed.astype(jnp.bfloat16)


def chip_index():
    return lax.axis_index("cz") * lax.axis_size("cy") + lax.axis_index("cy")


def shift_pairs(count, step):
    return [(i, (i - step) % count) for i in range(count)]


def gather_blocks(x, name):
    count = lax.axis_size(name)
    copies = jnp.broadcast_to(x[None], (count,) + x.shape)
    return lax.all_to_all(copies, name, 0, 0)


def spread_blocks(x, name):
    return lax.all_to_all(x, name, 0, 0)


def merge_parts(parts, heads_dev, value_dim):
    width = heads_dev * value_dim
    numer = parts[:, :, :width]
    peaks = parts[:, :, width : width + heads_dev]
    sums = parts[:, :, width + heads_dev :]
    peak = jnp.max(peaks, axis=0)
    shifted = jnp.where(jnp.isfinite(peak), peak, jnp.zeros_like(peak))
    scale = jnp.exp(peaks - shifted[None])
    count, rows = parts.shape[0], parts.shape[1]
    numer = numer.reshape(count, rows, heads_dev, value_dim) * scale[:, :, :, None]
    numer = jnp.sum(numer, axis=0).reshape(rows, width)
    total = jnp.sum(scale * sums, axis=0)
    return jnp.concatenate([numer, peak, total], axis=1)


def reduce_rows(x, heads_dev, value_dim):
    for name in ("cy", "cz"):
        count = lax.axis_size(name)
        blocks = x.reshape((count, x.shape[0] // count) + x.shape[1:])
        x = merge_parts(spread_blocks(blocks, name), heads_dev, value_dim)
    return x


def swap_cores(x):
    return lax.ppermute(x, CORE, [(0, 1), (1, 0)])


def body(q_nope, q_rope, w_uk, w_uv, cache, cache_scale, new_latent, cache_doc, new_lengths):
    tok_rows = q_nope.shape[0]
    heads_dev, nope_dim, latent_dim = w_uk.shape
    value_dim = w_uv.shape[2]
    rope_dim = q_rope.shape[1] // heads_dev
    cores = lax.axis_size(CORE)
    chips = 1
    for name in CHIP_PARTS:
        chips = chips * lax.axis_size(name)
    q_rows = tok_rows * chips
    my_chip = chip_index()
    my_core = lax.axis_index(CORE)
    other_core = 1 - my_core
    score_scale = (nope_dim + rope_dim) ** (-0.5)

    dequant = (cache.astype(jnp.float32) * cache_scale[:, None]).astype(jnp.bfloat16)
    own_keys = jnp.concatenate([dequant, new_latent], axis=0)
    other_keys = swap_cores(own_keys)
    other_doc = swap_cores(cache_doc)

    own_q = jnp.concatenate([q_nope, q_rope], axis=1)
    all_q = gather_blocks(own_q, "cz").reshape(-1, own_q.shape[1])
    all_q = gather_blocks(all_q, "cy").reshape(-1, own_q.shape[1])
    nope_width = heads_dev * nope_dim
    q_rot = all_q[:, nope_width:].reshape(q_rows, heads_dev, rope_dim).transpose(1, 0, 2)
    cache_len = cache.shape[0]
    block_len = cache_len // cache_doc.shape[0]
    row = jnp.arange(q_rows, dtype=jnp.int32)
    z_count = lax.axis_size("cz")
    row_chip = (row // tok_rows) % z_count * lax.axis_size("cy") + row // (tok_rows * z_count)
    query_pos = (row_chip * cores + my_core) * tok_rows + row % tok_rows
    query_doc = doc_index(query_pos, new_lengths)

    def key_meta(core, docs):
        new_pos = (my_chip * cores + core) * tok_rows + jnp.arange(tok_rows, dtype=jnp.int32)
        key_doc = jnp.concatenate([jnp.repeat(docs, block_len), doc_index(new_pos, new_lengths)])
        key_pos = jnp.concatenate([jnp.full((cache_len,), -1, dtype=jnp.int32), new_pos])
        return key_doc, key_pos

    own_doc, own_pos = key_meta(my_core, cache_doc)
    far_doc, far_pos = key_meta(other_core, other_doc)
    key_rows = jnp.concatenate([own_keys, other_keys], axis=0)
    key_doc = jnp.concatenate([own_doc, far_doc])
    key_pos = jnp.concatenate([own_pos, far_pos])
    numer, stats = attend(
        all_q, w_uk, q_rot, key_rows, w_uv,
        query_doc[:, None], query_pos[:, None], key_doc[None, :], key_pos[None, :], score_scale,
    )
    width = heads_dev * value_dim
    parts = jnp.concatenate([numer, stats[:, : 2 * heads_dev]], axis=1)
    merged = reduce_rows(parts, heads_dev, value_dim)
    own_numer = merged[:, :width].reshape(tok_rows, heads_dev, value_dim)
    own_total = merged[:, width + heads_dev :]
    result = own_numer / own_total[:, :, None]
    return result.astype(jnp.bfloat16).reshape(tok_rows, heads_dev * value_dim)


def solution(mesh):
    ctx_shape = (8, 4, 2)
    grid = np.asarray(mesh.devices).reshape(ctx_shape + (mesh.shape["wa"],))
    fine = Mesh(grid, CHIP_PARTS + (CORE, "wa"))
    rows = CHIP_PARTS + (CORE,)
    placed = (
        P(rows, "wa"),
        P(rows, "wa"),
        P("wa", None, None),
        P("wa", None, None),
        P(rows, None),
        P(rows),
        P(rows, None),
        P(rows),
        P(),
    )
    return jax.shard_map(
        body, mesh=fine, in_specs=placed, out_specs=P(rows, "wa"), check_vma=False
    )
```

```python
import jax
import jax.numpy as jnp
import numpy as np
from jax import lax
from jax.sharding import Mesh, PartitionSpec as P
import functools
from jax.experimental import pallas as pl
from jax.experimental.pallas import tpu as pltpu

CHIP_PARTS = ("cz", "cy")
CORE = "cc"


def attend_kernel(scale, latent, pack, q_nope_ref, w_uk_ref, q_rope_ref, keys_ref, w_uv_ref, qdoc_ref,
                  qpos_ref, kdoc_ref, kpos_ref, numer_ref, stats_ref, bias_ref):
    group = pl.program_id(0)
    heads = pl.num_programs(0) * pack

    @pl.when(group == 0)
    def _():
        allowed = (qdoc_ref[...] == kdoc_ref[...]) & (kpos_ref[...] <= qpos_ref[...])
        bias_ref[...] = jnp.where(allowed, 0.0, -jnp.inf)
        stats_ref[...] = jnp.zeros(stats_ref.shape, jnp.float32)

    nope = w_uk_ref.shape[1]
    rows = q_nope_ref.shape[0]
    q_lat = jnp.concatenate(
        [jnp.dot(q_nope_ref[:, j * nope : (j + 1) * nope], w_uk_ref[j], preferred_element_type=jnp.float32)
         for j in range(pack)],
        axis=0,
    ).astype(jnp.bfloat16)
    q_rot = jnp.concatenate([q_rope_ref[j] for j in range(pack)], axis=0)
    k_lat = keys_ref[:, :latent]
    nt = (((1,), (1,)), ((), ()))
    score = lax.dot_general(q_lat, k_lat, nt, preferred_element_type=jnp.float32)
    score = score + lax.dot_general(q_rot, keys_ref[:, latent:], nt, preferred_element_type=jnp.float32)
    bias = bias_ref[...]
    masked = jnp.concatenate(
        [score[j * rows : (j + 1) * rows] * scale + bias for j in range(pack)], axis=0
    )
    peak = jnp.max(masked, axis=1, keepdims=True)
    shift = jnp.where(peak > -jnp.inf, peak, 0.0)
    weight = jnp.exp(masked - shift)
    total = jnp.sum(weight, axis=1, keepdims=True)
    part = jnp.dot(weight.astype(jnp.bfloat16), k_lat, preferred_element_type=jnp.float32)
    part = part.astype(jnp.bfloat16)
    value = w_uv_ref.shape[2]
    lane = lax.broadcasted_iota(jnp.int32, stats_ref.shape, 1)
    stats = stats_ref[...]
    for j in range(pack):
        numer_ref[:, j * value : (j + 1) * value] = jnp.dot(
            part[j * rows : (j + 1) * rows], w_uv_ref[j], preferred_element_type=jnp.float32
        )
        head = group * pack + j
        stats = jnp.where(lane == head, peak[j * rows : (j + 1) * rows], stats)
        stats = jnp.where(lane == heads + head, total[j * rows : (j + 1) * rows], stats)
    stats_ref[...] = stats


def attend(all_q, w_uk, q_rope, keys, w_uv, qdoc, qpos, kdoc, kpos, scale, interpret=False):
    heads, nope, latent = w_uk.shape
    pack = 2
    rows = all_q.shape[0]
    rope = q_rope.shape[2]
    key_count, width = keys.shape
    value = w_uv.shape[2]
    return pl.pallas_call(
        functools.partial(attend_kernel, scale, latent, pack),
        grid=(heads // pack,),
        in_specs=[
            pl.BlockSpec((rows, pack * nope), lambda h: (0, h)),
            pl.BlockSpec((pack, nope, latent), lambda h: (h, 0, 0)),
            pl.BlockSpec((pack, rows, rope), lambda h: (h, 0, 0)),
            pl.BlockSpec((key_count, width), lambda h: (0, 0)),
            pl.BlockSpec((pack, latent, value), lambda h: (h, 0, 0)),
            pl.BlockSpec((rows, 1), lambda h: (0, 0)),
            pl.BlockSpec((rows, 1), lambda h: (0, 0)),
            pl.BlockSpec((1, key_count), lambda h: (0, 0)),
            pl.BlockSpec((1, key_count), lambda h: (0, 0)),
        ],
        out_specs=[
            pl.BlockSpec((rows, pack * value), lambda h: (0, h)),
            pl.BlockSpec((rows, 128), lambda h: (0, 0)),
        ],
        out_shape=[
            jax.ShapeDtypeStruct((rows, heads * value), jnp.float32),
            jax.ShapeDtypeStruct((rows, 128), jnp.float32),
        ],
        scratch_shapes=[pltpu.VMEM((rows, key_count), jnp.float32)],
        interpret=interpret,
    )(all_q, w_uk, q_rope, keys, w_uv, qdoc, qpos, kdoc, kpos)


def doc_index(position, new_lengths):
    ends = jnp.cumsum(new_lengths)
    return jnp.sum((ends[None, :] <= position[:, None]).astype(jnp.int32), axis=1)


def absorb_rows(nope_rows, w_uk):
    row_count = nope_rows.shape[0]
    heads_dev, nope_dim, latent_dim = w_uk.shape
    shaped = nope_rows.reshape(row_count, heads_dev, nope_dim)
    absorbed = jnp.einsum("thn,hnl->thl", shaped, w_uk, preferred_element_type=jnp.float32)
    return absorbed.astype(jnp.bfloat16)


def chip_index():
    return lax.axis_index("cz") * lax.axis_size("cy") + lax.axis_index("cy")


def shift_pairs(count, step):
    return [(i, (i - step) % count) for i in range(count)]


def gather_blocks(x, name):
    count = lax.axis_size(name)
    copies = jnp.broadcast_to(x[None], (count,) + x.shape)
    return lax.all_to_all(copies, name, 0, 0)


def spread_blocks(x, name):
    return lax.all_to_all(x, name, 0, 0)


def merge_parts(parts, heads_dev, value_dim):
    width = heads_dev * value_dim
    numer = parts[:, :, :width]
    peaks = parts[:, :, width : width + heads_dev]
    sums = parts[:, :, width + heads_dev :]
    peak = jnp.max(peaks, axis=0)
    shifted = jnp.where(jnp.isfinite(peak), peak, jnp.zeros_like(peak))
    scale = jnp.exp(peaks - shifted[None])
    count, rows = parts.shape[0], parts.shape[1]
    numer = numer.reshape(count, rows, heads_dev, value_dim) * scale[:, :, :, None]
    numer = jnp.sum(numer, axis=0).reshape(rows, width)
    total = jnp.sum(scale * sums, axis=0)
    return jnp.concatenate([numer, peak, total], axis=1)


def reduce_rows(x, heads_dev, value_dim):
    for name in ("cy", "cz"):
        count = lax.axis_size(name)
        blocks = x.reshape((count, x.shape[0] // count) + x.shape[1:])
        x = merge_parts(spread_blocks(blocks, name), heads_dev, value_dim)
    return x


def swap_cores(x):
    return lax.ppermute(x, CORE, [(0, 1), (1, 0)])


def body(q_nope, q_rope, w_uk, w_uv, cache, cache_scale, new_latent, cache_doc, new_lengths):
    tok_rows = q_nope.shape[0]
    heads_dev, nope_dim, latent_dim = w_uk.shape
    value_dim = w_uv.shape[2]
    rope_dim = q_rope.shape[1] // heads_dev
    cores = lax.axis_size(CORE)
    chips = 1
    for name in CHIP_PARTS:
        chips = chips * lax.axis_size(name)
    q_rows = tok_rows * chips
    my_chip = chip_index()
    my_core = lax.axis_index(CORE)
    other_core = 1 - my_core
    score_scale = (nope_dim + rope_dim) ** (-0.5)

    dequant = (cache.astype(jnp.float32) * cache_scale[:, None]).astype(jnp.bfloat16)
    own_keys = jnp.concatenate([dequant, new_latent], axis=0)
    other_keys = swap_cores(own_keys)
    other_doc = swap_cores(cache_doc)

    own_q = jnp.concatenate([q_nope, q_rope], axis=1)
    all_q = gather_blocks(own_q, "cz").reshape(-1, own_q.shape[1])
    all_q = gather_blocks(all_q, "cy").reshape(-1, own_q.shape[1])
    nope_width = heads_dev * nope_dim
    q_rot = all_q[:, nope_width:].reshape(q_rows, heads_dev, rope_dim).transpose(1, 0, 2)
    cache_len = cache.shape[0]
    block_len = cache_len // cache_doc.shape[0]
    row = jnp.arange(q_rows, dtype=jnp.int32)
    z_count = lax.axis_size("cz")
    row_chip = (row // tok_rows) % z_count * lax.axis_size("cy") + row // (tok_rows * z_count)
    query_pos = (row_chip * cores + my_core) * tok_rows + row % tok_rows
    query_doc = doc_index(query_pos, new_lengths)

    def key_meta(core, docs):
        new_pos = (my_chip * cores + core) * tok_rows + jnp.arange(tok_rows, dtype=jnp.int32)
        key_doc = jnp.concatenate([jnp.repeat(docs, block_len), doc_index(new_pos, new_lengths)])
        key_pos = jnp.concatenate([jnp.full((cache_len,), -1, dtype=jnp.int32), new_pos])
        return key_doc, key_pos

    own_doc, own_pos = key_meta(my_core, cache_doc)
    far_doc, far_pos = key_meta(other_core, other_doc)
    key_rows = jnp.concatenate([own_keys, other_keys], axis=0)
    key_doc = jnp.concatenate([own_doc, far_doc])
    key_pos = jnp.concatenate([own_pos, far_pos])
    numer, stats = attend(
        all_q, w_uk, q_rot, key_rows, w_uv,
        query_doc[:, None], query_pos[:, None], key_doc[None, :], key_pos[None, :], score_scale,
    )
    width = heads_dev * value_dim
    parts = jnp.concatenate([numer, stats[:, : 2 * heads_dev]], axis=1)
    merged = reduce_rows(parts, heads_dev, value_dim)
    own_numer = merged[:, :width].reshape(tok_rows, heads_dev, value_dim)
    own_total = merged[:, width + heads_dev :]
    result = own_numer / own_total[:, :, None]
    return result.astype(jnp.bfloat16).reshape(tok_rows, heads_dev * value_dim)


def solution(mesh):
    ctx_shape = (8, 4, 2)
    grid = np.asarray(mesh.devices).reshape(ctx_shape + (mesh.shape["wa"],))
    fine = Mesh(grid, CHIP_PARTS + (CORE, "wa"))
    rows = CHIP_PARTS + (CORE,)
    placed = (
        P(rows, "wa"),
        P(rows, "wa"),
        P("wa", None, None),
        P("wa", None, None),
        P(rows, None),
        P(rows),
        P(rows, None),
        P(rows),
        P(),
    )
    return jax.shard_map(
        body, mesh=fine, in_specs=placed, out_specs=P(rows, "wa"), check_vma=False
    )
```

```python
import jax
import jax.numpy as jnp
import numpy as np
from jax import lax
from jax.sharding import Mesh, PartitionSpec as P
import functools
from jax.experimental import pallas as pl
from jax.experimental.pallas import tpu as pltpu

CHIP_PARTS = ("cz", "cy")
CORE = "cc"


def attend_kernel(scale, latent, pack, q_nope_ref, w_uk_ref, q_rope_ref, keys_ref, w_uv_ref, qdoc_ref,
                  qpos_ref, kdoc_ref, kpos_ref, numer_ref, stats_ref, bias_ref):
    group = pl.program_id(0)
    heads = pl.num_programs(0) * pack

    @pl.when(group == 0)
    def _():
        allowed = (qdoc_ref[...] == kdoc_ref[...]) & (kpos_ref[...] <= qpos_ref[...])
        bias_ref[...] = jnp.where(allowed, 0.0, -jnp.inf)
        stats_ref[...] = jnp.zeros(stats_ref.shape, jnp.float32)

    nope = w_uk_ref.shape[1]
    rows = q_nope_ref.shape[0]
    q_lat = jnp.concatenate(
        [jnp.dot(q_nope_ref[:, j * nope : (j + 1) * nope], w_uk_ref[j], preferred_element_type=jnp.float32)
         for j in range(pack)],
        axis=0,
    ).astype(jnp.bfloat16)
    q_rot = jnp.concatenate([q_rope_ref[j] for j in range(pack)], axis=0)
    k_lat = keys_ref[:, :latent]
    nt = (((1,), (1,)), ((), ()))
    score = lax.dot_general(q_lat, k_lat, nt, preferred_element_type=jnp.float32)
    score = score + lax.dot_general(q_rot, keys_ref[:, latent:], nt, preferred_element_type=jnp.float32)
    bias = bias_ref[...]
    masked = jnp.concatenate(
        [score[j * rows : (j + 1) * rows] * scale + bias for j in range(pack)], axis=0
    )
    peak = jnp.max(masked, axis=1, keepdims=True)
    shift = jnp.where(peak > -jnp.inf, peak, 0.0)
    weight = jnp.exp(masked - shift)
    total = jnp.sum(weight, axis=1, keepdims=True)
    part = jnp.dot(weight.astype(jnp.bfloat16), k_lat, preferred_element_type=jnp.float32)
    part = part.astype(jnp.bfloat16)
    value = w_uv_ref.shape[2]
    lane = lax.broadcasted_iota(jnp.int32, stats_ref.shape, 1)
    stats = stats_ref[...]
    for j in range(pack):
        numer_ref[:, j * value : (j + 1) * value] = jnp.dot(
            part[j * rows : (j + 1) * rows], w_uv_ref[j], preferred_element_type=jnp.float32
        )
        head = group * pack + j
        stats = jnp.where(lane == head, peak[j * rows : (j + 1) * rows], stats)
        stats = jnp.where(lane == heads + head, total[j * rows : (j + 1) * rows], stats)
    stats_ref[...] = stats


def attend(all_q, w_uk, q_rope, keys, w_uv, qdoc, qpos, kdoc, kpos, scale, interpret=False):
    heads, nope, latent = w_uk.shape
    pack = 4
    rows = all_q.shape[0]
    rope = q_rope.shape[2]
    key_count, width = keys.shape
    value = w_uv.shape[2]
    return pl.pallas_call(
        functools.partial(attend_kernel, scale, latent, pack),
        grid=(heads // pack,),
        in_specs=[
            pl.BlockSpec((rows, pack * nope), lambda h: (0, h)),
            pl.BlockSpec((pack, nope, latent), lambda h: (h, 0, 0)),
            pl.BlockSpec((pack, rows, rope), lambda h: (h, 0, 0)),
            pl.BlockSpec((key_count, width), lambda h: (0, 0)),
            pl.BlockSpec((pack, latent, value), lambda h: (h, 0, 0)),
            pl.BlockSpec((rows, 1), lambda h: (0, 0)),
            pl.BlockSpec((rows, 1), lambda h: (0, 0)),
            pl.BlockSpec((1, key_count), lambda h: (0, 0)),
            pl.BlockSpec((1, key_count), lambda h: (0, 0)),
        ],
        out_specs=[
            pl.BlockSpec((rows, pack * value), lambda h: (0, h)),
            pl.BlockSpec((rows, 128), lambda h: (0, 0)),
        ],
        out_shape=[
            jax.ShapeDtypeStruct((rows, heads * value), jnp.float32),
            jax.ShapeDtypeStruct((rows, 128), jnp.float32),
        ],
        scratch_shapes=[pltpu.VMEM((rows, key_count), jnp.float32)],
        interpret=interpret,
    )(all_q, w_uk, q_rope, keys, w_uv, qdoc, qpos, kdoc, kpos)


def doc_index(position, new_lengths):
    ends = jnp.cumsum(new_lengths)
    return jnp.sum((ends[None, :] <= position[:, None]).astype(jnp.int32), axis=1)


def absorb_rows(nope_rows, w_uk):
    row_count = nope_rows.shape[0]
    heads_dev, nope_dim, latent_dim = w_uk.shape
    shaped = nope_rows.reshape(row_count, heads_dev, nope_dim)
    absorbed = jnp.einsum("thn,hnl->thl", shaped, w_uk, preferred_element_type=jnp.float32)
    return absorbed.astype(jnp.bfloat16)


def chip_index():
    return lax.axis_index("cz") * lax.axis_size("cy") + lax.axis_index("cy")


def shift_pairs(count, step):
    return [(i, (i - step) % count) for i in range(count)]


def gather_blocks(x, name):
    count = lax.axis_size(name)
    copies = jnp.broadcast_to(x[None], (count,) + x.shape)
    return lax.all_to_all(copies, name, 0, 0)


def spread_blocks(x, name):
    return lax.all_to_all(x, name, 0, 0)


def merge_parts(parts, heads_dev, value_dim):
    width = heads_dev * value_dim
    numer = parts[:, :, :width]
    peaks = parts[:, :, width : width + heads_dev]
    sums = parts[:, :, width + heads_dev :]
    peak = jnp.max(peaks, axis=0)
    shifted = jnp.where(jnp.isfinite(peak), peak, jnp.zeros_like(peak))
    scale = jnp.exp(peaks - shifted[None])
    count, rows = parts.shape[0], parts.shape[1]
    numer = numer.reshape(count, rows, heads_dev, value_dim) * scale[:, :, :, None]
    numer = jnp.sum(numer, axis=0).reshape(rows, width)
    total = jnp.sum(scale * sums, axis=0)
    return jnp.concatenate([numer, peak, total], axis=1)


def reduce_rows(x, heads_dev, value_dim):
    for name in ("cy", "cz"):
        count = lax.axis_size(name)
        blocks = x.reshape((count, x.shape[0] // count) + x.shape[1:])
        x = merge_parts(spread_blocks(blocks, name), heads_dev, value_dim)
    return x


def swap_cores(x):
    return lax.ppermute(x, CORE, [(0, 1), (1, 0)])


def body(q_nope, q_rope, w_uk, w_uv, cache, cache_scale, new_latent, cache_doc, new_lengths):
    tok_rows = q_nope.shape[0]
    heads_dev, nope_dim, latent_dim = w_uk.shape
    value_dim = w_uv.shape[2]
    rope_dim = q_rope.shape[1] // heads_dev
    cores = lax.axis_size(CORE)
    chips = 1
    for name in CHIP_PARTS:
        chips = chips * lax.axis_size(name)
    q_rows = tok_rows * chips
    my_chip = chip_index()
    my_core = lax.axis_index(CORE)
    other_core = 1 - my_core
    score_scale = (nope_dim + rope_dim) ** (-0.5)

    dequant = (cache.astype(jnp.float32) * cache_scale[:, None]).astype(jnp.bfloat16)
    own_keys = jnp.concatenate([dequant, new_latent], axis=0)
    other_keys = swap_cores(own_keys)
    other_doc = swap_cores(cache_doc)

    own_q = jnp.concatenate([q_nope, q_rope], axis=1)
    all_q = gather_blocks(own_q, "cz").reshape(-1, own_q.shape[1])
    all_q = gather_blocks(all_q, "cy").reshape(-1, own_q.shape[1])
    nope_width = heads_dev * nope_dim
    q_rot = all_q[:, nope_width:].reshape(q_rows, heads_dev, rope_dim).transpose(1, 0, 2)
    cache_len = cache.shape[0]
    block_len = cache_len // cache_doc.shape[0]
    row = jnp.arange(q_rows, dtype=jnp.int32)
    z_count = lax.axis_size("cz")
    row_chip = (row // tok_rows) % z_count * lax.axis_size("cy") + row // (tok_rows * z_count)
    query_pos = (row_chip * cores + my_core) * tok_rows + row % tok_rows
    query_doc = doc_index(query_pos, new_lengths)

    def key_meta(core, docs):
        new_pos = (my_chip * cores + core) * tok_rows + jnp.arange(tok_rows, dtype=jnp.int32)
        key_doc = jnp.concatenate([jnp.repeat(docs, block_len), doc_index(new_pos, new_lengths)])
        key_pos = jnp.concatenate([jnp.full((cache_len,), -1, dtype=jnp.int32), new_pos])
        return key_doc, key_pos

    own_doc, own_pos = key_meta(my_core, cache_doc)
    far_doc, far_pos = key_meta(other_core, other_doc)
    key_rows = jnp.concatenate([own_keys, other_keys], axis=0)
    key_doc = jnp.concatenate([own_doc, far_doc])
    key_pos = jnp.concatenate([own_pos, far_pos])
    numer, stats = attend(
        all_q, w_uk, q_rot, key_rows, w_uv,
        query_doc[:, None], query_pos[:, None], key_doc[None, :], key_pos[None, :], score_scale,
    )
    width = heads_dev * value_dim
    parts = jnp.concatenate([numer, stats[:, : 2 * heads_dev]], axis=1)
    merged = reduce_rows(parts, heads_dev, value_dim)
    own_numer = merged[:, :width].reshape(tok_rows, heads_dev, value_dim)
    own_total = merged[:, width + heads_dev :]
    result = own_numer / own_total[:, :, None]
    return result.astype(jnp.bfloat16).reshape(tok_rows, heads_dev * value_dim)


def solution(mesh):
    ctx_shape = (8, 4, 2)
    grid = np.asarray(mesh.devices).reshape(ctx_shape + (mesh.shape["wa"],))
    fine = Mesh(grid, CHIP_PARTS + (CORE, "wa"))
    rows = CHIP_PARTS + (CORE,)
    placed = (
        P(rows, "wa"),
        P(rows, "wa"),
        P("wa", None, None),
        P("wa", None, None),
        P(rows, None),
        P(rows),
        P(rows, None),
        P(rows),
        P(),
    )
    return jax.shard_map(
        body, mesh=fine, in_specs=placed, out_specs=P(rows, "wa"), check_vma=False
    )
```
